32 devices in a mesh: day: 8 (over z, x), pt: 4 (over y, core).
Axes of the slice: x: 2, y: 2, z: 4, core: 2. Of those that a mesh axis runs over, the one named last changes fastest.
Arguments:
- points: bfloat16 [8, 64, 2048], P('day', None, 'pt'), may hold values from -0.45 to 0.45
- cells: bfloat16 [8, 64, 8192], P('day', None, 'pt'), may hold values from -0.44921875 to 0.44921875
- clone_weight: float32 [8, 64, 2048], P('day', None, 'pt'), may hold values from 0.1 to 1
- potential: float32 [8, 2048], P('day', 'pt'), may hold values from 0.2 to 5
- support_count: int32 [8], P('day'), may hold values from 512 to 2048, as said below
- cell_count: int32 [8], P('day'), may hold values from 2048 to 8192, as said below
Outputs:
- forward_message: float32 [8, 64, 2048], P('day', None, 'pt')
- backward_message: float32 [8, 64, 2048], P('day', None, 'pt')
- fit_ratio: float32 [8, 2048], P('day', 'pt')
The draws below stay inside these ranges and needn't reach their ends.
Inputs may be any that keep to these rules, and one draw needn't show every extreme that they name: Live support points of a day are its first support_count slots; some day has all 2048 slots live and some day has 512. Observed cells of a day are its first cell_count slots; some day fills all 8192 slots and some day has 2048.
All inputs are finite; a program needn't handle non-finite values.
Results may differ from the reference program's by a relative error of at most 0.0003.
Values may be sent and summed in bfloat16 or wider, within the bound.
No kernel may reach another device: no remote copies, remote signals or barrier semaphores. Data moves between devices by JAX's collectives and lax.ppermute only.
A program may use at most 64 MiB of HBM per device.

```python
import jax
import jax.numpy as jnp
from jax import lax

D = 64
C = 64
DAYS = 8
PTS = 2048
OBS = 8192


def pick_counts(key, slots):
    first_key, second_key = jax.random.split(key)
    drawn = jax.random.randint(first_key, (DAYS,), slots // 4, slots + 1)
    order = jax.random.permutation(second_key, DAYS)
    drawn = drawn.at[order[0]].set(slots)
    drawn = drawn.at[order[1]].set(slots // 4)
    return drawn.astype(jnp.int32)


def draw_support_count(key, part):
    return pick_counts(jax.random.fold_in(key, 11), PTS)


def draw_cell_count(key, part):
    return pick_counts(jax.random.fold_in(key, 23), OBS)


def slot_parity():
    return (jnp.arange(PTS, dtype=jnp.int32) % 2).astype(jnp.float32)


def draw_points(key, part):
    jitter_key = jax.random.fold_in(key, 37)
    cluster_sign = 1.0 - 2.0 * slot_parity()
    jitter = 0.08 * jnp.clip(jax.random.normal(jitter_key, (DAYS, D, PTS), jnp.float32), -3.0, 3.0)
    centre = 0.2
    values = centre * cluster_sign[None, None, :] + jitter
    return jnp.clip(values, -0.45, 0.45).astype(jnp.bfloat16)


def draw_clone_weight(key, part):
    cluster_key = jax.random.fold_in(key, 41)
    entry_key = jax.random.fold_in(key, 43)
    parity = slot_parity()
    grouped = jax.random.uniform(cluster_key, (DAYS, C, 2), jnp.float32)
    entries = jax.random.uniform(entry_key, (DAYS, C, PTS), jnp.float32)
    chosen = grouped[:, :, 0:1] * (1.0 - parity)[None, None, :] + grouped[:, :, 1:2] * parity[None, None, :]
    exponent = -1.0 + 0.4 * chosen + 0.6 * entries
    return jnp.exp(exponent * 2.302585093).astype(jnp.float32)


def draw_potential(key, part):
    cluster_key = jax.random.fold_in(key, 47)
    entry_key = jax.random.fold_in(key, 53)
    parity = slot_parity()
    grouped = jax.random.uniform(cluster_key, (DAYS, 2), jnp.float32, -1.0, 1.0)
    entries = jax.random.uniform(entry_key, (DAYS, PTS), jnp.float32, -1.0, 1.0)
    chosen = grouped[:, 0:1] * (1.0 - parity)[None, :] + grouped[:, 1:2] * parity[None, :]
    exponent = 0.6 * chosen + 0.8 * entries
    return jnp.exp(exponent).astype(jnp.float32)


def levels(rng, shape, pieces, least, top_value):
    def one(dim, blocks):
        heights = jax.random.uniform(jax.random.fold_in(jax.random.fold_in(rng, 6), dim), (blocks,), jnp.float32, least / len(pieces), top_value / len(pieces))
        return jnp.repeat(jnp.exp(heights), shape[dim] // blocks).reshape((-1,) + (1,) * (len(shape) - dim - 1))

    factor_of = one(*pieces[0])
    for cut in pieces[1:]:
        factor_of = factor_of * one(*cut)
    return factor_of


def setup_inputs(seed: int = 0) -> dict:
    streams_of = jax.random.split(jax.random.key(seed), 7)
    return {
        "points": draw_points(jax.random.fold_in(streams_of[6], 71), 0),
        "cells": jnp.clip(jax.random.uniform(streams_of[1], (DAYS, D, OBS), jnp.float32, -0.44921875, 0.44921875) * levels(streams_of[1], (DAYS, D, OBS), ((0, 8), (2, 4)), -0.4, 0.0), -0.44921875, 0.44921875).astype(jnp.bfloat16),
        "clone_weight": draw_clone_weight(jax.random.fold_in(streams_of[6], 71), 0),
        "potential": draw_potential(jax.random.fold_in(streams_of[6], 71), 0),
        "support_count": draw_support_count(jax.random.fold_in(streams_of[6], 71), 0),
        "cell_count": draw_cell_count(jax.random.fold_in(streams_of[6], 71), 0),
    }


def squared_dist(left_pts, right_pts):
    left_wide = left_pts.astype(jnp.float32)
    right_wide = right_pts.astype(jnp.float32)
    left_norm = jnp.sum(left_wide * left_wide, axis=0)
    right_norm = jnp.sum(right_wide * right_wide, axis=0)
    inner = lax.dot_general(left_pts, right_pts, (((0,), (0,)), ((), ())), preferred_element_type=jnp.float32)
    return left_norm[:, None] + right_norm[None, :] - 2.0 * inner


def settle(values, live_next, day_total):
    masked = values * live_next[None, :]
    return masked * day_total / jnp.sum(masked, axis=1, keepdims=True)


def advance(message, inputs):
    source_pts, target_pts, source_weight, live_next, day_total = inputs
    sent_rows = (message * source_weight).astype(jnp.bfloat16)
    chain_kernel = jnp.exp(-squared_dist(source_pts, target_pts)).astype(jnp.bfloat16)
    advanced = settle(jnp.dot(sent_rows, chain_kernel, preferred_element_type=jnp.float32), live_next, day_total)
    return advanced, advanced


def reference(points, cells, clone_weight, potential, support_count, cell_count):
    support_total = points.shape[2]
    cell_slots = cells.shape[2]
    clones = clone_weight.shape[1]
    positions = jnp.arange(support_total, dtype=jnp.int32)
    live_rows = (positions[None, :] < support_count[:, None]).astype(jnp.float32)
    weight = clone_weight * potential[:, None, :]
    day_totals = support_count.astype(jnp.float32)
    first_message = jnp.broadcast_to(live_rows[0][None, :], (clones, support_total))
    ignored, later = lax.scan(advance, first_message, (points[:-1], points[1:], weight[:-1], live_rows[1:], day_totals[1:]))
    forward_message = jnp.concatenate([first_message[None], later], axis=0)
    final_message = jnp.broadcast_to(live_rows[-1][None, :], (clones, support_total))
    ignored_too, earlier = lax.scan(advance, final_message, (points[1:], points[:-1], weight[1:], live_rows[:-1], day_totals[:-1]), reverse=True)
    backward_message = jnp.concatenate([earlier, final_message[None]], axis=0)
    mass_rows = live_rows * potential * jnp.sum(forward_message * clone_weight * backward_message, axis=1)

    def fit_day(inputs):
        day_pts, day_cells, day_mass, day_live, cell_total = inputs
        fit_kernel = jnp.exp(-squared_dist(day_pts, day_cells))
        density = jnp.dot(day_mass, fit_kernel, precision=lax.Precision.HIGHEST) / jnp.sum(day_mass)
        cell_live = (jnp.arange(cell_slots, dtype=jnp.int32) < cell_total).astype(jnp.float32)
        summed = jnp.dot(fit_kernel, cell_live / density, precision=lax.Precision.HIGHEST)
        return day_live / cell_total.astype(jnp.float32) * summed

    fit_ratio = lax.map(fit_day, (points, cells, mass_rows, live_rows, cell_count))
    return forward_message, backward_message, fit_ratio
```

```python
import jax
import jax.numpy as jnp
from jax import lax
from jax.sharding import PartitionSpec as P


def shifted(block, axis, distance):
    devices = range(lax.axis_size(axis))
    route = [(i - distance, i) for i in devices if i - distance in devices]
    return lax.ppermute(block, axis, route)


def norm_of(coords):
    wide = coords.astype(jnp.float32)
    return jnp.sum(wide * wide, axis=0)


def squared_dist(left_pts, left_norm, right_pts, right_norm):
    inner = lax.dot_general(
        left_pts, right_pts, (((0,), (0,)), ((), ())), preferred_element_type=jnp.float32
    )
    return left_norm[:, None] + right_norm[None, :] - 2.0 * inner


def shards(points, cells, clone_weight, potential, support_count, cell_count):
    pt_rank = lax.axis_index("pt")
    day_index = lax.axis_index("day")
    day_count = lax.axis_size("day")
    own_pts = points[0]
    per_device = own_pts.shape[1]
    day_pts = lax.all_gather(own_pts, "pt", axis=1, tiled=True)
    before_pts = shifted(day_pts, "day", 1)
    after_pts = shifted(day_pts, "day", -1)
    support_total = day_pts.shape[1]
    block_cw = lax.all_to_all(clone_weight[0], "pt", 0, 1, tiled=True)
    full_pot = lax.all_gather(potential[0], "pt", axis=0, tiled=True)
    block_weight = block_cw * full_pot[None, :]
    block_rows = block_cw.shape[0]
    live_total = support_count[0].astype(jnp.float32)
    live_all = (jnp.arange(support_total, dtype=jnp.int32) < support_count[0]).astype(jnp.float32)
    live_own = lax.dynamic_slice_in_dim(live_all, pt_rank * per_device, per_device)
    day_norm = norm_of(day_pts)
    forward_kernel = jnp.exp(
        -squared_dist(before_pts, norm_of(before_pts), day_pts, day_norm)
    ).astype(jnp.bfloat16)
    backward_kernel = jnp.exp(
        -squared_dist(after_pts, norm_of(after_pts), day_pts, day_norm)
    ).astype(jnp.bfloat16)

    def settle(values):
        masked = values * live_all[None, :]
        return masked * live_total / jnp.sum(masked, axis=1, keepdims=True)

    seed_rows = jnp.broadcast_to(live_all[None, :], (block_rows, support_total))
    forward_rows = seed_rows
    backward_rows = seed_rows
    for step in range(day_count - 1):
        forward_in = shifted((forward_rows * block_weight).astype(jnp.bfloat16), "day", 1)
        backward_in = shifted((backward_rows * block_weight).astype(jnp.bfloat16), "day", -1)
        forward_new = settle(
            jnp.dot(forward_in, forward_kernel, preferred_element_type=jnp.float32)
        )
        backward_new = settle(
            jnp.dot(backward_in, backward_kernel, preferred_element_type=jnp.float32)
        )
        forward_rows = jnp.where(day_index == step + 1, forward_new, forward_rows)
        backward_rows = jnp.where(day_index == day_count - 2 - step, backward_new, backward_rows)

    forward_out = lax.all_to_all(forward_rows, "pt", 1, 0, tiled=True)
    backward_out = lax.all_to_all(backward_rows, "pt", 1, 0, tiled=True)
    mass_part = jnp.sum(forward_rows * block_cw * backward_rows, axis=0)
    full_mass = live_all * full_pot * lax.psum(mass_part, "pt")
    mass_total = jnp.sum(full_mass)

    cell_total = cell_count[0]
    cell_total_f = cell_total.astype(jnp.float32)
    own_cells = cells[0]
    own_slots = own_cells.shape[1]
    cell_norm = norm_of(own_cells)
    fit_kernel = jnp.exp(-squared_dist(day_pts, day_norm, own_cells, cell_norm))
    density = jnp.sum(full_mass[:, None] * fit_kernel, axis=0) / mass_total
    cell_live = (pt_rank * own_slots + jnp.arange(own_slots, dtype=jnp.int32) < cell_total).astype(
        jnp.float32
    )
    inverse = cell_live / density
    ratio_rows = jnp.sum(fit_kernel * inverse[None, :], axis=1)
    summed = lax.psum_scatter(ratio_rows, "pt", scatter_dimension=0, tiled=True)
    fit_rows_out = live_own / cell_total_f * summed
    return (forward_out[None], backward_out[None], fit_rows_out[None])


def solution(mesh):
    in_specs = (
        P("day", None, "pt"),
        P("day", None, "pt"),
        P("day", None, "pt"),
        P("day", "pt"),
        P("day"),
        P("day"),
    )
    out_specs = (P("day", None, "pt"), P("day", None, "pt"), P("day", "pt"))
    return jax.shard_map(shards, mesh=mesh, in_specs=in_specs, out_specs=out_specs, check_vma=False)
```

```python
import jax
import jax.numpy as jnp
from jax import lax
from jax.sharding import PartitionSpec as P


def shifted(block, axis, distance):
    devices = range(lax.axis_size(axis))
    route = [(i - distance, i) for i in devices if i - distance in devices]
    return lax.ppermute(block, axis, route)


def norm_of(coords):
    wide = coords.astype(jnp.float32)
    return jnp.sum(wide * wide, axis=0)


def squared_dist(left_pts, left_norm, right_pts, right_norm):
    inner = lax.dot_general(
        left_pts, right_pts, (((0,), (0,)), ((), ())), preferred_element_type=jnp.float32
    )
    return left_norm[:, None] + right_norm[None, :] - 2.0 * inner


def shards(points, cells, clone_weight, potential, support_count, cell_count):
    pt_rank = lax.axis_index("pt")
    day_index = lax.axis_index("day")
    day_count = lax.axis_size("day")
    own_pts = points[0]
    per_device = own_pts.shape[1]
    day_pts = lax.all_gather(own_pts, "pt", axis=1, tiled=True)
    before_pts = shifted(day_pts, "day", 1)
    after_pts = shifted(day_pts, "day", -1)
    support_total = day_pts.shape[1]
    block_cw = lax.all_to_all(clone_weight[0], "pt", 0, 1, tiled=True)
    full_pot = lax.all_gather(potential[0], "pt", axis=0, tiled=True)
    block_weight = block_cw * full_pot[None, :]
    block_rows = block_cw.shape[0]
    live_total = support_count[0].astype(jnp.float32)
    live_all = (jnp.arange(support_total, dtype=jnp.int32) < support_count[0]).astype(jnp.float32)
    live_own = lax.dynamic_slice_in_dim(live_all, pt_rank * per_device, per_device)
    day_norm = norm_of(day_pts)
    source_pts = jnp.stack([before_pts, after_pts])
    source_norm = jnp.stack([norm_of(before_pts), norm_of(after_pts)])
    inner = lax.dot_general(
        source_pts, day_pts, (((1,), (0,)), ((), ())), preferred_element_type=jnp.float32
    )
    chain_kernel = jnp.exp(
        -(source_norm[:, :, None] + day_norm[None, None, :] - 2.0 * inner)
    ).astype(jnp.bfloat16)

    def settle(values):
        masked = values * live_all[None, None, :]
        return masked * live_total / jnp.sum(masked, axis=2, keepdims=True)

    seed_rows = jnp.broadcast_to(live_all[None, None, :], (2, block_rows, support_total))
    rows = seed_rows
    for step in range(day_count - 1):
        sent = (rows * block_weight[None]).astype(jnp.bfloat16)
        arrived = jnp.stack([shifted(sent[0], "day", 1), shifted(sent[1], "day", -1)])
        fresh = settle(
            lax.dot_general(
                arrived,
                chain_kernel,
                (((2,), (1,)), ((0,), (0,))),
                preferred_element_type=jnp.float32,
            )
        )
        keep = jnp.stack([day_index == step + 1, day_index == day_count - 2 - step])
        rows = jnp.where(keep[:, None, None], fresh, rows)
    forward_rows = rows[0]
    backward_rows = rows[1]

    forward_out = lax.all_to_all(forward_rows, "pt", 1, 0, tiled=True)
    backward_out = lax.all_to_all(backward_rows, "pt", 1, 0, tiled=True)
    mass_part = jnp.sum(forward_rows * block_cw * backward_rows, axis=0)
    full_mass = live_all * full_pot * lax.psum(mass_part, "pt")
    mass_total = jnp.sum(full_mass)

    cell_total = cell_count[0]
    cell_total_f = cell_total.astype(jnp.float32)
    own_cells = cells[0]
    own_slots = own_cells.shape[1]
    cell_norm = norm_of(own_cells)
    fit_kernel = jnp.exp(-squared_dist(day_pts, day_norm, own_cells, cell_norm))
    density = jnp.sum(full_mass[:, None] * fit_kernel, axis=0) / mass_total
    cell_live = (pt_rank * own_slots + jnp.arange(own_slots, dtype=jnp.int32) < cell_total).astype(
        jnp.float32
    )
    inverse = cell_live / density
    ratio_rows = jnp.sum(fit_kernel * inverse[None, :], axis=1)
    summed = lax.psum_scatter(ratio_rows, "pt", scatter_dimension=0, tiled=True)
    fit_rows_out = live_own / cell_total_f * summed
    return (forward_out[None], backward_out[None], fit_rows_out[None])


def solution(mesh):
    in_specs = (
        P("day", None, "pt"),
        P("day", None, "pt"),
        P("day", None, "pt"),
        P("day", "pt"),
        P("day"),
        P("day"),
    )
    out_specs = (P("day", None, "pt"), P("day", None, "pt"), P("day", "pt"))
    return jax.shard_map(shards, mesh=mesh, in_specs=in_specs, out_specs=out_specs, check_vma=False)
```

```python
import jax
import jax.numpy as jnp
from jax import lax
from jax.sharding import PartitionSpec as P


def shifted(block, axis, distance):
    devices = range(lax.axis_size(axis))
    route = [(i - distance, i) for i in devices if i - distance in devices]
    return lax.ppermute(block, axis, route)


def norm_of(coords):
    wide = coords.astype(jnp.float32)
    return jnp.sum(wide * wide, axis=0)


def squared_dist(left_pts, left_norm, right_pts, right_norm):
    inner = lax.dot_general(
        left_pts, right_pts, (((0,), (0,)), ((), ())), preferred_element_type=jnp.float32
    )
    return left_norm[:, None] + right_norm[None, :] - 2.0 * inner


def shards(points, cells, clone_weight, potential, support_count, cell_count):
    pt_rank = lax.axis_index("pt")
    day_index = lax.axis_index("day")
    day_count = lax.axis_size("day")
    own_pts = points[0]
    per_device = own_pts.shape[1]
    day_pts = lax.all_gather(own_pts, "pt", axis=1, tiled=True)
    before_pts = shifted(day_pts, "day", 1)
    after_pts = shifted(day_pts, "day", -1)
    support_total = day_pts.shape[1]
    own_weight = clone_weight[0] * potential[0][None, :]
    block_weight = lax.all_to_all(own_weight, "pt", 0, 1, tiled=True)
    block_rows = block_weight.shape[0]
    live_total = support_count[0].astype(jnp.float32)
    live_all = (jnp.arange(support_total, dtype=jnp.int32) < support_count[0]).astype(jnp.float32)
    live_own = lax.dynamic_slice_in_dim(live_all, pt_rank * per_device, per_device)
    day_norm = norm_of(day_pts)
    source_pts = jnp.stack([before_pts, after_pts])
    source_norm = jnp.stack([norm_of(before_pts), norm_of(after_pts)])
    inner = lax.dot_general(
        source_pts, day_pts, (((1,), (0,)), ((), ())), preferred_element_type=jnp.float32
    )
    chain_kernel = jnp.exp(
        -(source_norm[:, :, None] + day_norm[None, None, :] - 2.0 * inner)
    ).astype(jnp.bfloat16)

    def settle(values):
        masked = values * live_all[None, None, :]
        return masked * live_total / jnp.sum(masked, axis=2, keepdims=True)

    seed_rows = jnp.broadcast_to(live_all[None, None, :], (2, block_rows, support_total))
    rows = seed_rows
    for step in range(day_count - 1):
        forward_from = step
        backward_from = day_count - 1 - step
        sent = (rows * block_weight[None]).astype(jnp.bfloat16)
        if forward_from != backward_from:
            outgoing = jnp.where(day_index == forward_from, sent[0], sent[1])
            route = [(forward_from, forward_from + 1), (backward_from, backward_from - 1)]
            incoming = lax.ppermute(outgoing, "day", route)
            arrived = jnp.stack([incoming, incoming])
        else:
            arrived = jnp.stack([shifted(sent[0], "day", 1), shifted(sent[1], "day", -1)])
        fresh = settle(
            lax.dot_general(
                arrived,
                chain_kernel,
                (((2,), (1,)), ((0,), (0,))),
                preferred_element_type=jnp.float32,
            )
        )
        keep = jnp.stack([day_index == step + 1, day_index == day_count - 2 - step])
        rows = jnp.where(keep[:, None, None], fresh, rows)
    forward_rows = rows[0]
    backward_rows = rows[1]

    forward_out = lax.all_to_all(forward_rows, "pt", 1, 0, tiled=True)
    backward_out = lax.all_to_all(backward_rows, "pt", 1, 0, tiled=True)
    mass_part = jnp.sum(forward_rows * block_weight * backward_rows, axis=0)
    full_mass = live_all * lax.psum(mass_part, "pt")
    mass_total = jnp.sum(full_mass)

    cell_total = cell_count[0]
    cell_total_f = cell_total.astype(jnp.float32)
    own_cells = cells[0]
    own_slots = own_cells.shape[1]
    cell_norm = norm_of(own_cells)
    fit_kernel = jnp.exp(-squared_dist(day_pts, day_norm, own_cells, cell_norm))
    density = jnp.sum(full_mass[:, None] * fit_kernel, axis=0) / mass_total
    cell_live = (pt_rank * own_slots + jnp.arange(own_slots, dtype=jnp.int32) < cell_total).astype(
        jnp.float32
    )
    inverse = cell_live / density
    ratio_rows = jnp.sum(fit_kernel * inverse[None, :], axis=1)
    summed = lax.psum_scatter(ratio_rows, "pt", scatter_dimension=0, tiled=True)
    fit_rows_out = live_own / cell_total_f * summed
    return (forward_out[None], backward_out[None], fit_rows_out[None])


def solution(mesh):
    in_specs = (
        P("day", None, "pt"),
        P("day", None, "pt"),
        P("day", None, "pt"),
        P("day", "pt"),
        P("day"),
        P("day"),
    )
    out_specs = (P("day", None, "pt"), P("day", None, "pt"), P("day", "pt"))
    return jax.shard_map(shards, mesh=mesh, in_specs=in_specs, out_specs=out_specs, check_vma=False)
```

```python
import jax
import jax.numpy as jnp
from jax import lax
from jax.sharding import PartitionSpec as P


def shifted(block, axis, distance):
    devices = range(lax.axis_size(axis))
    route = [(i - distance, i) for i in devices if i - distance in devices]
    return lax.ppermute(block, axis, route)


def norm_of(coords):
    wide = coords.astype(jnp.float32)
    return jnp.sum(wide * wide, axis=0)


def squared_dist(left_pts, left_norm, right_pts, right_norm):
    inner = lax.dot_general(
        left_pts, right_pts, (((0,), (0,)), ((), ())), preferred_element_type=jnp.float32
    )
    return left_norm[:, None] + right_norm[None, :] - 2.0 * inner


def shards(points, cells, clone_weight, potential, support_count, cell_count):
    pt_rank = lax.axis_index("pt")
    day_index = lax.axis_index("day")
    day_count = lax.axis_size("day")
    own_pts = points[0]
    per_device = own_pts.shape[1]
    day_pts = lax.all_gather(own_pts, "pt", axis=1, tiled=True)
    support_total = day_pts.shape[1]
    own_weight = clone_weight[0] * potential[0][None, :]
    block_weight = lax.all_to_all(own_weight, "pt", 0, 1, tiled=True)
    block_rows = block_weight.shape[0]
    live_total = support_count[0].astype(jnp.float32)
    live_all = (jnp.arange(support_total, dtype=jnp.int32) < support_count[0]).astype(jnp.float32)
    live_own = lax.dynamic_slice_in_dim(live_all, pt_rank * per_device, per_device)
    day_norm = norm_of(day_pts)

    def chain_kernel(source_pts):
        dist = squared_dist(source_pts, norm_of(source_pts), day_pts, day_norm)
        return jnp.exp(-dist).astype(jnp.bfloat16)

    half = day_count // 2
    switch_step = half - 1
    first_forward = day_index < half
    first_route = [(d - 1, d) for d in range(1, half)]
    first_route += [(d + 1, d) for d in range(half, day_count - 1)]
    first_kernel = chain_kernel(lax.ppermute(day_pts, "day", first_route))

    def settle(values):
        masked = values * live_all[None, :]
        return masked * live_total / jnp.sum(masked, axis=1, keepdims=True)

    rows = jnp.broadcast_to(live_all[None, None, :], (2, block_rows, support_total))
    later_kernel = None
    for step in range(day_count - 1):
        if step == min(1, switch_step):
            later_pts, rows = lax.optimization_barrier((day_pts, rows))
            later_source = jnp.where(
                first_forward,
                lax.ppermute(later_pts, "day", [(d + 1, d) for d in range(half)]),
                lax.ppermute(later_pts, "day", [(d - 1, d) for d in range(half, day_count)]),
            )
        if step == switch_step:
            later_source, rows = lax.optimization_barrier((later_source, rows))
            later_kernel = chain_kernel(later_source)
        kernel = first_kernel if step < switch_step else later_kernel
        forward_from = step
        backward_from = day_count - 1 - step
        sent = (rows * block_weight[None]).astype(jnp.bfloat16)
        outgoing = jnp.where(day_index == forward_from, sent[0], sent[1])
        route = [(forward_from, forward_from + 1), (backward_from, backward_from - 1)]
        incoming = lax.ppermute(outgoing, "day", route)
        fresh = settle(jnp.dot(incoming, kernel, preferred_element_type=jnp.float32))
        keep = jnp.stack([day_index == step + 1, day_index == day_count - 2 - step])
        rows = jnp.where(keep[:, None, None], fresh[None], rows)
    forward_rows = rows[0]
    backward_rows = rows[1]
    both_out = lax.all_to_all(rows, "pt", 2, 1, tiled=True)
    forward_out = both_out[0]
    backward_out = both_out[1]
    mass_part = jnp.sum(forward_rows * block_weight * backward_rows, axis=0)
    full_mass = live_all * lax.psum(mass_part, "pt")
    mass_total = jnp.sum(full_mass)

    cell_total = cell_count[0]
    cell_total_f = cell_total.astype(jnp.float32)
    own_cells = cells[0]
    own_slots = own_cells.shape[1]
    cell_norm = norm_of(own_cells)
    fit_kernel = jnp.exp(-squared_dist(day_pts, day_norm, own_cells, cell_norm))
    density = jnp.sum(full_mass[:, None] * fit_kernel, axis=0) / mass_total
    cell_live = (pt_rank * own_slots + jnp.arange(own_slots, dtype=jnp.int32) < cell_total).astype(
        jnp.float32
    )
    inverse = cell_live / density
    ratio_rows = jnp.sum(fit_kernel * inverse[None, :], axis=1)
    summed = lax.psum_scatter(ratio_rows, "pt", scatter_dimension=0, tiled=True)
    fit_rows_out = live_own / cell_total_f * summed
    return (forward_out[None], backward_out[None], fit_rows_out[None])


def solution(mesh):
    in_specs = (
        P("day", None, "pt"),
        P("day", None, "pt"),
        P("day", None, "pt"),
        P("day", "pt"),
        P("day"),
        P("day"),
    )
    out_specs = (P("day", None, "pt"), P("day", None, "pt"), P("day", "pt"))
    return jax.shard_map(shards, mesh=mesh, in_specs=in_specs, out_specs=out_specs, check_vma=False)
```

```python
import jax
import jax.numpy as jnp
from jax import lax
from jax.sharding import PartitionSpec as P


def shifted(block, axis, distance):
    devices = range(lax.axis_size(axis))
    route = [(i - distance, i) for i in devices if i - distance in devices]
    return lax.ppermute(block, axis, route)


def norm_of(coords):
    wide = coords.astype(jnp.float32)
    return jnp.sum(wide * wide, axis=0)


def squared_dist(left_pts, left_norm, right_pts, right_norm):
    inner = lax.dot_general(
        left_pts, right_pts, (((0,), (0,)), ((), ())), preferred_element_type=jnp.float32
    )
    return left_norm[:, None] + right_norm[None, :] - 2.0 * inner


def shards(points, cells, clone_weight, potential, support_count, cell_count):
    pt_rank = lax.axis_index("pt")
    day_index = lax.axis_index("day")
    day_count = lax.axis_size("day")
    own_pts = points[0]
    per_device = own_pts.shape[1]
    day_pts = lax.all_gather(own_pts, "pt", axis=1, tiled=True)
    support_total = day_pts.shape[1]
    own_weight = clone_weight[0] * potential[0][None, :]
    full_weight = lax.all_gather(own_weight, "pt", axis=1, tiled=True)
    block_rows = full_weight.shape[0] // lax.axis_size("pt")
    block_weight = lax.dynamic_slice_in_dim(full_weight, pt_rank * block_rows, block_rows, 0)
    live_total = support_count[0].astype(jnp.float32)
    live_all = (jnp.arange(support_total, dtype=jnp.int32) < support_count[0]).astype(jnp.float32)
    live_own = lax.dynamic_slice_in_dim(live_all, pt_rank * per_device, per_device)
    day_norm = norm_of(day_pts)

    def chain_kernel(source_pts):
        dist = squared_dist(source_pts, norm_of(source_pts), day_pts, day_norm)
        return jnp.exp(-dist).astype(jnp.bfloat16)

    half = day_count // 2
    switch_step = half - 1
    first_forward = day_index < half
    first_route = [(d - 1, d) for d in range(1, half)]
    first_route += [(d + 1, d) for d in range(half, day_count - 1)]
    first_kernel = chain_kernel(lax.ppermute(day_pts, "day", first_route))

    def settle(values):
        masked = values * live_all[None, :]
        return masked * live_total / jnp.sum(masked, axis=1, keepdims=True)

    rows = jnp.broadcast_to(live_all[None, None, :], (2, block_rows, support_total))
    later_kernel = None
    for step in range(day_count - 1):
        if step == min(1, switch_step):
            later_pts, rows = lax.optimization_barrier((day_pts, rows))
            later_source = jnp.where(
                first_forward,
                lax.ppermute(later_pts, "day", [(d + 1, d) for d in range(half)]),
                lax.ppermute(later_pts, "day", [(d - 1, d) for d in range(half, day_count)]),
            )
        if step == switch_step:
            later_source, rows = lax.optimization_barrier((later_source, rows))
            later_kernel = chain_kernel(later_source)
        kernel = first_kernel if step < switch_step else later_kernel
        forward_from = step
        backward_from = day_count - 1 - step
        sent = (rows * block_weight[None]).astype(jnp.bfloat16)
        outgoing = jnp.where(day_index == forward_from, sent[0], sent[1])
        route = [(forward_from, forward_from + 1), (backward_from, backward_from - 1)]
        incoming = lax.ppermute(outgoing, "day", route)
        fresh = settle(jnp.dot(incoming, kernel, preferred_element_type=jnp.float32))
        keep = jnp.stack([day_index == step + 1, day_index == day_count - 2 - step])
        rows = jnp.where(keep[:, None, None], fresh[None], rows)
    every_rows = lax.all_gather(rows, "pt", axis=1, tiled=True)
    full_mass = live_all * jnp.sum(every_rows[0] * full_weight * every_rows[1], axis=0)
    own_rows = lax.dynamic_slice_in_dim(every_rows, pt_rank * per_device, per_device, 2)
    forward_out = own_rows[0]
    backward_out = own_rows[1]
    mass_total = jnp.sum(full_mass)

    cell_total = cell_count[0]
    cell_total_f = cell_total.astype(jnp.float32)
    own_cells = cells[0]
    own_slots = own_cells.shape[1]
    cell_norm = norm_of(own_cells)
    fit_kernel = jnp.exp(-squared_dist(day_pts, day_norm, own_cells, cell_norm))
    density = jnp.sum(full_mass[:, None] * fit_kernel, axis=0) / mass_total
    cell_live = (pt_rank * own_slots + jnp.arange(own_slots, dtype=jnp.int32) < cell_total).astype(
        jnp.float32
    )
    inverse = cell_live / density
    ratio_rows = jnp.sum(fit_kernel * inverse[None, :], axis=1)
    summed = lax.psum_scatter(ratio_rows, "pt", scatter_dimension=0, tiled=True)
    fit_rows_out = live_own / cell_total_f * summed
    return (forward_out[None], backward_out[None], fit_rows_out[None])


def solution(mesh):
    in_specs = (
        P("day", None, "pt"),
        P("day", None, "pt"),
        P("day", None, "pt"),
        P("day", "pt"),
        P("day"),
        P("day"),
    )
    out_specs = (P("day", None, "pt"), P("day", None, "pt"), P("day", "pt"))
    return jax.shard_map(shards, mesh=mesh, in_specs=in_specs, out_specs=out_specs, check_vma=False)
```

```python
import jax
import jax.numpy as jnp
from jax import lax
from jax.sharding import PartitionSpec as P


def shifted(block, axis, distance):
    devices = range(lax.axis_size(axis))
    route = [(i - distance, i) for i in devices if i - distance in devices]
    return lax.ppermute(block, axis, route)


def swap_blocks(x, take_axis, put_axis, put_shape):
    count = lax.axis_size("pt")
    rank = lax.axis_index("pt")
    take = x.shape[take_axis] // count
    put = put_shape[put_axis] // count
    out = jnp.zeros(put_shape, x.dtype)
    for shift in range(count):
        piece = lax.dynamic_slice_in_dim(x, ((rank + shift) % count) * take, take, take_axis)
        if shift:
            piece = lax.ppermute(piece, "pt", [(i, (i + shift) % count) for i in range(count)])
        out = lax.dynamic_update_slice_in_dim(out, piece, ((rank - shift) % count) * put, put_axis)
    return out


def norm_of(coords):
    wide = coords.astype(jnp.float32)
    return jnp.sum(wide * wide, axis=0)


def squared_dist(left_pts, left_norm, right_pts, right_norm):
    inner = lax.dot_general(
        left_pts, right_pts, (((0,), (0,)), ((), ())), preferred_element_type=jnp.float32
    )
    return left_norm[:, None] + right_norm[None, :] - 2.0 * inner


def shards(points, cells, clone_weight, potential, support_count, cell_count):
    pt_rank = lax.axis_index("pt")
    day_index = lax.axis_index("day")
    day_count = lax.axis_size("day")
    own_pts = points[0]
    per_device = own_pts.shape[1]
    day_pts = lax.all_gather(own_pts, "pt", axis=1, tiled=True)
    support_total = day_pts.shape[1]
    own_weight = clone_weight[0] * potential[0][None, :]
    block_rows = own_weight.shape[0] // lax.axis_size("pt")
    block_weight = swap_blocks(own_weight, 0, 1, (block_rows, day_pts.shape[1]))
    live_total = support_count[0].astype(jnp.float32)
    live_all = (jnp.arange(support_total, dtype=jnp.int32) < support_count[0]).astype(jnp.float32)
    live_own = lax.dynamic_slice_in_dim(live_all, pt_rank * per_device, per_device)
    day_norm = norm_of(day_pts)

    def chain_kernel(source_pts):
        dist = squared_dist(source_pts, norm_of(source_pts), day_pts, day_norm)
        return jnp.exp(-dist).astype(jnp.bfloat16)

    half = day_count // 2
    switch_step = half - 1
    first_forward = day_index < half
    first_route = [(d - 1, d) for d in range(1, half)]
    first_route += [(d + 1, d) for d in range(half, day_count - 1)]
    first_kernel = chain_kernel(lax.ppermute(day_pts, "day", first_route))

    def settle(values):
        masked = values * live_all[None, :]
        return masked * live_total / jnp.sum(masked, axis=1, keepdims=True)

    rows = jnp.broadcast_to(live_all[None, None, :], (2, block_rows, support_total))
    later_kernel = None
    for step in range(day_count - 1):
        if step == min(1, switch_step):
            later_pts, rows = lax.optimization_barrier((day_pts, rows))
            later_source = jnp.where(
                first_forward,
                lax.ppermute(later_pts, "day", [(d + 1, d) for d in range(half)]),
                lax.ppermute(later_pts, "day", [(d - 1, d) for d in range(half, day_count)]),
            )
        if step == switch_step:
            later_source, rows = lax.optimization_barrier((later_source, rows))
            later_kernel = chain_kernel(later_source)
        kernel = first_kernel if step < switch_step else later_kernel
        forward_from = step
        backward_from = day_count - 1 - step
        sent = (rows * block_weight[None]).astype(jnp.bfloat16)
        outgoing = jnp.where(day_index == forward_from, sent[0], sent[1])
        route = [(forward_from, forward_from + 1), (backward_from, backward_from - 1)]
        incoming = lax.ppermute(outgoing, "day", route)
        fresh = settle(jnp.dot(incoming, kernel, preferred_element_type=jnp.float32))
        keep = jnp.stack([day_index == step + 1, day_index == day_count - 2 - step])
        rows = jnp.where(keep[:, None, None], fresh[None], rows)
    forward_rows = rows[0]
    backward_rows = rows[1]
    both_out = swap_blocks(rows, 2, 1, (2, own_weight.shape[0], per_device))
    forward_out = both_out[0]
    backward_out = both_out[1]
    mass_part = jnp.sum(forward_rows * block_weight * backward_rows, axis=0)
    full_mass = live_all * lax.psum(mass_part, "pt")
    mass_total = jnp.sum(full_mass)

    cell_total = cell_count[0]
    cell_total_f = cell_total.astype(jnp.float32)
    own_cells = cells[0]
    own_slots = own_cells.shape[1]
    cell_norm = norm_of(own_cells)
    fit_kernel = jnp.exp(-squared_dist(day_pts, day_norm, own_cells, cell_norm))
    density = jnp.sum(full_mass[:, None] * fit_kernel, axis=0) / mass_total
    cell_live = (pt_rank * own_slots + jnp.arange(own_slots, dtype=jnp.int32) < cell_total).astype(
        jnp.float32
    )
    inverse = cell_live / density
    ratio_rows = jnp.sum(fit_kernel * inverse[None, :], axis=1)
    summed = lax.psum_scatter(ratio_rows, "pt", scatter_dimension=0, tiled=True)
    fit_rows_out = live_own / cell_total_f * summed
    return (forward_out[None], backward_out[None], fit_rows_out[None])


def solution(mesh):
    in_specs = (
        P("day", None, "pt"),
        P("day", None, "pt"),
        P("day", None, "pt"),
        P("day", "pt"),
        P("day"),
        P("day"),
    )
    out_specs = (P("day", None, "pt"), P("day", None, "pt"), P("day", "pt"))
    return jax.shard_map(shards, mesh=mesh, in_specs=in_specs, out_specs=out_specs, check_vma=False)
```

```python
import jax
import jax.numpy as jnp
from jax import lax
from jax.sharding import PartitionSpec as P


def shifted(block, axis, distance):
    devices = range(lax.axis_size(axis))
    route = [(i - distance, i) for i in devices if i - distance in devices]
    return lax.ppermute(block, axis, route)


def swap_blocks(x, take_axis, put_axis, put_shape):
    count = lax.axis_size("pt")
    rank = lax.axis_index("pt")
    take = x.shape[take_axis] // count
    put = put_shape[put_axis] // count
    out = jnp.zeros(put_shape, x.dtype)
    for shift in range(count):
        piece = lax.dynamic_slice_in_dim(x, ((rank + shift) % count) * take, take, take_axis)
        if shift:
            piece = lax.ppermute(piece, "pt", [(i, (i + shift) % count) for i in range(count)])
        out = lax.dynamic_update_slice_in_dim(out, piece, ((rank - shift) % count) * put, put_axis)
    return out


def sum_over_pt(x):
    count = lax.axis_size("pt")
    every = swap_blocks(jnp.broadcast_to(x[None], (count,) + x.shape), 0, 0, (count,) + x.shape)
    return jnp.sum(every, axis=0)


def sum_scatter_over_pt(x):
    count = lax.axis_size("pt")
    every = swap_blocks(x, 0, 0, x.shape)
    return jnp.sum(every.reshape((count, x.shape[0] // count) + x.shape[1:]), axis=0)


def norm_of(coords):
    wide = coords.astype(jnp.float32)
    return jnp.sum(wide * wide, axis=0)


def squared_dist(left_pts, left_norm, right_pts, right_norm):
    inner = lax.dot_general(
        left_pts, right_pts, (((0,), (0,)), ((), ())), preferred_element_type=jnp.float32
    )
    return left_norm[:, None] + right_norm[None, :] - 2.0 * inner


def shards(points, cells, clone_weight, potential, support_count, cell_count):
    pt_rank = lax.axis_index("pt")
    day_index = lax.axis_index("day")
    day_count = lax.axis_size("day")
    own_pts = points[0]
    per_device = own_pts.shape[1]
    day_pts = lax.all_gather(own_pts, "pt", axis=1, tiled=True)
    support_total = day_pts.shape[1]
    own_weight = clone_weight[0] * potential[0][None, :]
    block_rows = own_weight.shape[0] // lax.axis_size("pt")
    block_weight = swap_blocks(own_weight, 0, 1, (block_rows, day_pts.shape[1]))
    live_total = support_count[0].astype(jnp.float32)
    live_all = (jnp.arange(support_total, dtype=jnp.int32) < support_count[0]).astype(jnp.float32)
    live_own = lax.dynamic_slice_in_dim(live_all, pt_rank * per_device, per_device)
    day_norm = norm_of(day_pts)

    def chain_kernel(source_pts):
        dist = squared_dist(source_pts, norm_of(source_pts), day_pts, day_norm)
        return jnp.exp(-dist).astype(jnp.bfloat16)

    half = day_count // 2
    switch_step = half - 1
    first_forward = day_index < half
    first_route = [(d - 1, d) for d in range(1, half)]
    first_route += [(d + 1, d) for d in range(half, day_count - 1)]
    first_kernel = chain_kernel(lax.ppermute(day_pts, "day", first_route))

    def settle(values):
        masked = values * live_all[None, :]
        return masked * live_total / jnp.sum(masked, axis=1, keepdims=True)

    rows = jnp.broadcast_to(live_all[None, None, :], (2, block_rows, support_total))
    later_kernel = None
    for step in range(day_count - 1):
        if step == min(1, switch_step):
            later_pts, rows = lax.optimization_barrier((day_pts, rows))
            later_source = jnp.where(
                first_forward,
                lax.ppermute(later_pts, "day", [(d + 1, d) for d in range(half)]),
                lax.ppermute(later_pts, "day", [(d - 1, d) for d in range(half, day_count)]),
            )
        if step == switch_step:
            later_source, rows = lax.optimization_barrier((later_source, rows))
            later_kernel = chain_kernel(later_source)
        kernel = first_kernel if step < switch_step else later_kernel
        forward_from = step
        backward_from = day_count - 1 - step
        sent = (rows * block_weight[None]).astype(jnp.bfloat16)
        outgoing = jnp.where(day_index == forward_from, sent[0], sent[1])
        route = [(forward_from, forward_from + 1), (backward_from, backward_from - 1)]
        incoming = lax.ppermute(outgoing, "day", route)
        fresh = settle(jnp.dot(incoming, kernel, preferred_element_type=jnp.float32))
        keep = jnp.stack([day_index == step + 1, day_index == day_count - 2 - step])
        rows = jnp.where(keep[:, None, None], fresh[None], rows)
    forward_rows = rows[0]
    backward_rows = rows[1]
    both_out = swap_blocks(rows, 2, 1, (2, own_weight.shape[0], per_device))
    forward_out = both_out[0]
    backward_out = both_out[1]
    mass_part = jnp.sum(forward_rows * block_weight * backward_rows, axis=0)
    full_mass = live_all * sum_over_pt(mass_part)
    mass_total = jnp.sum(full_mass)

    cell_total = cell_count[0]
    cell_total_f = cell_total.astype(jnp.float32)
    own_cells = cells[0]
    own_slots = own_cells.shape[1]
    cell_norm = norm_of(own_cells)
    fit_kernel = jnp.exp(-squared_dist(day_pts, day_norm, own_cells, cell_norm))
    density = jnp.sum(full_mass[:, None] * fit_kernel, axis=0) / mass_total
    cell_live = (pt_rank * own_slots + jnp.arange(own_slots, dtype=jnp.int32) < cell_total).astype(
        jnp.float32
    )
    inverse = cell_live / density
    ratio_rows = jnp.sum(fit_kernel * inverse[None, :], axis=1)
    summed = sum_scatter_over_pt(ratio_rows)
    fit_rows_out = live_own / cell_total_f * summed
    return (forward_out[None], backward_out[None], fit_rows_out[None])


def solution(mesh):
    in_specs = (
        P("day", None, "pt"),
        P("day", None, "pt"),
        P("day", None, "pt"),
        P("day", "pt"),
        P("day"),
        P("day"),
    )
    out_specs = (P("day", None, "pt"), P("day", None, "pt"), P("day", "pt"))
    return jax.shard_map(shards, mesh=mesh, in_specs=in_specs, out_specs=out_specs, check_vma=False)
```

```python
import jax
import jax.numpy as jnp
from jax import lax
from jax.sharding import PartitionSpec as P


def shifted(block, axis, distance):
    devices = range(lax.axis_size(axis))
    route = [(i - distance, i) for i in devices if i - distance in devices]
    return lax.ppermute(block, axis, route)


def swap_blocks(x, take_axis, put_axis, put_shape):
    count = lax.axis_size("pt")
    rank = lax.axis_index("pt")
    take = x.shape[take_axis] // count
    put = put_shape[put_axis] // count
    out = jnp.zeros(put_shape, x.dtype)
    for shift in range(count):
        piece = lax.dynamic_slice_in_dim(x, ((rank + shift) % count) * take, take, take_axis)
        if shift:
            piece = lax.ppermute(piece, "pt", [(i, (i + shift) % count) for i in range(count)])
        out = lax.dynamic_update_slice_in_dim(out, piece, ((rank - shift) % count) * put, put_axis)
    return out


def sum_over_pt(x):
    count = lax.axis_size("pt")
    every = swap_blocks(jnp.broadcast_to(x[None], (count,) + x.shape), 0, 0, (count,) + x.shape)
    return jnp.sum(every, axis=0)


def sum_scatter_over_pt(x):
    count = lax.axis_size("pt")
    every = swap_blocks(x, 0, 0, x.shape)
    return jnp.sum(every.reshape((count, x.shape[0] // count) + x.shape[1:]), axis=0)


def norm_of(coords):
    wide = coords.astype(jnp.float32)
    return jnp.sum(wide * wide, axis=0)


def squared_dist(left_pts, left_norm, right_pts, right_norm):
    inner = lax.dot_general(
        left_pts, right_pts, (((0,), (0,)), ((), ())), preferred_element_type=jnp.float32
    )
    return left_norm[:, None] + right_norm[None, :] - 2.0 * inner


def shards(points, cells, clone_weight, potential, support_count, cell_count):
    pt_rank = lax.axis_index("pt")
    day_index = lax.axis_index("day")
    day_count = lax.axis_size("day")
    own_pts = points[0]
    per_device = own_pts.shape[1]
    day_pts = lax.all_gather(own_pts, "pt", axis=1, tiled=True)
    support_total = day_pts.shape[1]
    own_weight = clone_weight[0] * potential[0][None, :]
    block_rows = own_weight.shape[0] // lax.axis_size("pt")
    block_weight = swap_blocks(own_weight, 0, 1, (block_rows, day_pts.shape[1]))
    live_total = support_count[0].astype(jnp.float32)
    live_all = (jnp.arange(support_total, dtype=jnp.int32) < support_count[0]).astype(jnp.float32)
    live_own = lax.dynamic_slice_in_dim(live_all, pt_rank * per_device, per_device)
    day_norm = norm_of(day_pts)

    def chain_kernel(source_pts):
        dist = squared_dist(source_pts, norm_of(source_pts), day_pts, day_norm)
        return jnp.exp(-dist).astype(jnp.bfloat16)

    half = day_count // 2
    switch_step = half - 1
    first_forward = day_index < half
    first_route = [(d - 1, d) for d in range(1, half)]
    first_route += [(d + 1, d) for d in range(half, day_count - 1)]
    first_kernel = chain_kernel(lax.ppermute(day_pts, "day", first_route))

    def settle(values):
        masked = values * live_all[None, :]
        return masked * live_total / jnp.sum(masked, axis=1, keepdims=True)

    rows = jnp.broadcast_to(live_all[None, None, :], (2, block_rows, support_total))
    later_kernel = None
    for step in range(day_count - 1):
        if step == min(1, switch_step):
            later_pts = lax.optimization_barrier((day_pts, rows))[0]
            later_source = jnp.where(
                first_forward,
                lax.ppermute(later_pts, "day", [(d + 1, d) for d in range(half)]),
                lax.ppermute(later_pts, "day", [(d - 1, d) for d in range(half, day_count)]),
            )
        if step == switch_step:
            later_source = lax.optimization_barrier((later_source, rows))[0]
            later_kernel = chain_kernel(later_source)
        kernel = first_kernel if step < switch_step else later_kernel
        forward_from = step
        backward_from = day_count - 1 - step
        sent = (rows * block_weight[None]).astype(jnp.bfloat16)
        outgoing = jnp.where(day_index == forward_from, sent[0], sent[1])
        route = [(forward_from, forward_from + 1), (backward_from, backward_from - 1)]
        incoming = lax.ppermute(outgoing, "day", route)
        fresh = settle(jnp.dot(incoming, kernel, preferred_element_type=jnp.float32))
        keep = jnp.stack([day_index == step + 1, day_index == day_count - 2 - step])
        rows = jnp.where(keep[:, None, None], fresh[None], rows)
    forward_rows = rows[0]
    backward_rows = rows[1]
    both_out = swap_blocks(rows, 2, 1, (2, own_weight.shape[0], per_device))
    forward_out = both_out[0]
    backward_out = both_out[1]
    mass_part = jnp.sum(forward_rows * block_weight * backward_rows, axis=0)
    full_mass = live_all * sum_over_pt(mass_part)
    mass_total = jnp.sum(full_mass)

    cell_total = cell_count[0]
    cell_total_f = cell_total.astype(jnp.float32)
    own_cells = cells[0]
    own_slots = own_cells.shape[1]
    cell_norm = norm_of(own_cells)
    fit_kernel = jnp.exp(-squared_dist(day_pts, day_norm, own_cells, cell_norm))
    density = jnp.sum(full_mass[:, None] * fit_kernel, axis=0) / mass_total
    cell_live = (pt_rank * own_slots + jnp.arange(own_slots, dtype=jnp.int32) < cell_total).astype(
        jnp.float32
    )
    inverse = cell_live / density
    ratio_rows = jnp.sum(fit_kernel * inverse[None, :], axis=1)
    summed = sum_scatter_over_pt(ratio_rows)
    fit_rows_out = live_own / cell_total_f * summed
    return (forward_out[None], backward_out[None], fit_rows_out[None])


def solution(mesh):
    in_specs = (
        P("day", None, "pt"),
        P("day", None, "pt"),
        P("day", None, "pt"),
        P("day", "pt"),
        P("day"),
        P("day"),
    )
    out_specs = (P("day", None, "pt"), P("day", None, "pt"), P("day", "pt"))
    return jax.shard_map(shards, mesh=mesh, in_specs=in_specs, out_specs=out_specs, check_vma=False)
```

```python
import jax
import jax.numpy as jnp
from jax import lax
from jax.sharding import PartitionSpec as P


def shifted(block, axis, distance):
    devices = range(lax.axis_size(axis))
    route = [(i - distance, i) for i in devices if i - distance in devices]
    return lax.ppermute(block, axis, route)


def swap_blocks(x, take_axis, put_axis, put_shape):
    count = lax.axis_size("pt")
    rank = lax.axis_index("pt")
    take = x.shape[take_axis] // count
    put = put_shape[put_axis] // count
    out = jnp.zeros(put_shape, x.dtype)
    for shift in range(count):
        piece = lax.dynamic_slice_in_dim(x, ((rank + shift) % count) * take, take, take_axis)
        if shift:
            piece = lax.ppermute(piece, "pt", [(i, (i + shift) % count) for i in range(count)])
        out = lax.dynamic_update_slice_in_dim(out, piece, ((rank - shift) % count) * put, put_axis)
    return out


def sum_over_pt(x):
    count = lax.axis_size("pt")
    every = swap_blocks(jnp.broadcast_to(x[None], (count,) + x.shape), 0, 0, (count,) + x.shape)
    return jnp.sum(every, axis=0)


def sum_scatter_over_pt(x):
    count = lax.axis_size("pt")
    every = swap_blocks(x, 0, 0, x.shape)
    return jnp.sum(every.reshape((count, x.shape[0] // count) + x.shape[1:]), axis=0)


def norm_of(coords):
    wide = coords.astype(jnp.float32)
    return jnp.sum(wide * wide, axis=0)


def squared_dist(left_pts, left_norm, right_pts, right_norm):
    inner = lax.dot_general(
        left_pts, right_pts, (((0,), (0,)), ((), ())), preferred_element_type=jnp.float32
    )
    return left_norm[:, None] + right_norm[None, :] - 2.0 * inner


def shards(points, cells, clone_weight, potential, support_count, cell_count):
    pt_rank = lax.axis_index("pt")
    day_index = lax.axis_index("day")
    day_count = lax.axis_size("day")
    own_pts = points[0]
    per_device = own_pts.shape[1]
    day_pts = lax.all_gather(own_pts, "pt", axis=1, tiled=True)
    support_total = day_pts.shape[1]
    own_weight = clone_weight[0] * potential[0][None, :]
    block_rows = own_weight.shape[0] // lax.axis_size("pt")
    block_weight = swap_blocks(own_weight, 0, 1, (block_rows, day_pts.shape[1]))
    live_total = support_count[0].astype(jnp.float32)
    live_all = (jnp.arange(support_total, dtype=jnp.int32) < support_count[0]).astype(jnp.float32)
    live_own = lax.dynamic_slice_in_dim(live_all, pt_rank * per_device, per_device)
    day_norm = norm_of(day_pts)

    def chain_kernel(source_pts):
        dist = squared_dist(source_pts, norm_of(source_pts), day_pts, day_norm)
        return jnp.exp(-dist).astype(jnp.bfloat16)

    half = day_count // 2
    switch_step = half - 1
    first_forward = day_index < half
    first_route = [(d - 1, d) for d in range(1, half)]
    first_route += [(d + 1, d) for d in range(half, day_count - 1)]
    first_kernel = chain_kernel(lax.ppermute(day_pts, "day", first_route))

    def settle(values):
        masked = values * live_all[None, :]
        return masked * live_total / jnp.sum(masked, axis=1, keepdims=True)

    rows = jnp.broadcast_to(live_all[None, None, :], (2, block_rows, support_total))
    later_kernel = None
    for step in range(day_count - 1):
        if step == min(1, switch_step):
            later_pts, rows = lax.optimization_barrier((day_pts, rows))
            later_source = jnp.where(
                first_forward,
                lax.ppermute(later_pts, "day", [(d + 1, d) for d in range(half)]),
                lax.ppermute(later_pts, "day", [(d - 1, d) for d in range(half, day_count)]),
            )
        if step == switch_step:
            later_source = lax.optimization_barrier((later_source, rows))[0]
            later_kernel = chain_kernel(later_source)
        kernel = first_kernel if step < switch_step else later_kernel
        forward_from = step
        backward_from = day_count - 1 - step
        sent = (rows * block_weight[None]).astype(jnp.bfloat16)
        outgoing = jnp.where(day_index == forward_from, sent[0], sent[1])
        route = [(forward_from, forward_from + 1), (backward_from, backward_from - 1)]
        incoming = lax.ppermute(outgoing, "day", route)
        fresh = settle(jnp.dot(incoming, kernel, preferred_element_type=jnp.float32))
        keep = jnp.stack([day_index == step + 1, day_index == day_count - 2 - step])
        rows = jnp.where(keep[:, None, None], fresh[None], rows)
    forward_rows = rows[0]
    backward_rows = rows[1]
    both_out = swap_blocks(rows, 2, 1, (2, own_weight.shape[0], per_device))
    forward_out = both_out[0]
    backward_out = both_out[1]
    mass_part = jnp.sum(forward_rows * block_weight * backward_rows, axis=0)
    full_mass = live_all * sum_over_pt(mass_part)
    mass_total = jnp.sum(full_mass)

    cell_total = cell_count[0]
    cell_total_f = cell_total.astype(jnp.float32)
    own_cells = cells[0]
    own_slots = own_cells.shape[1]
    cell_norm = norm_of(own_cells)
    fit_kernel = jnp.exp(-squared_dist(day_pts, day_norm, own_cells, cell_norm))
    density = jnp.sum(full_mass[:, None] * fit_kernel, axis=0) / mass_total
    cell_live = (pt_rank * own_slots + jnp.arange(own_slots, dtype=jnp.int32) < cell_total).astype(
        jnp.float32
    )
    inverse = cell_live / density
    ratio_rows = jnp.sum(fit_kernel * inverse[None, :], axis=1)
    summed = sum_scatter_over_pt(ratio_rows)
    fit_rows_out = live_own / cell_total_f * summed
    return (forward_out[None], backward_out[None], fit_rows_out[None])


def solution(mesh):
    in_specs = (
        P("day", None, "pt"),
        P("day", None, "pt"),
        P("day", None, "pt"),
        P("day", "pt"),
        P("day"),
        P("day"),
    )
    out_specs = (P("day", None, "pt"), P("day", None, "pt"), P("day", "pt"))
    return jax.shard_map(shards, mesh=mesh, in_specs=in_specs, out_specs=out_specs, check_vma=False)
```

```python
import jax
import jax.numpy as jnp
from jax import lax
from jax.sharding import PartitionSpec as P


def shifted(block, axis, distance):
    devices = range(lax.axis_size(axis))
    route = [(i - distance, i) for i in devices if i - distance in devices]
    return lax.ppermute(block, axis, route)


def swap_blocks(x, take_axis, put_axis, put_shape):
    count = lax.axis_size("pt")
    rank = lax.axis_index("pt")
    take = x.shape[take_axis] // count
    put = put_shape[put_axis] // count
    out = jnp.zeros(put_shape, x.dtype)
    for shift in range(count):
        piece = lax.dynamic_slice_in_dim(x, ((rank + shift) % count) * take, take, take_axis)
        if shift:
            piece = lax.ppermute(piece, "pt", [(i, (i + shift) % count) for i in range(count)])
        out = lax.dynamic_update_slice_in_dim(out, piece, ((rank - shift) % count) * put, put_axis)
    return out


def sum_over_pt(x):
    count = lax.axis_size("pt")
    every = swap_blocks(jnp.broadcast_to(x[None], (count,) + x.shape), 0, 0, (count,) + x.shape)
    return jnp.sum(every, axis=0)


def sum_scatter_over_pt(x):
    count = lax.axis_size("pt")
    every = swap_blocks(x, 0, 0, x.shape)
    return jnp.sum(every.reshape((count, x.shape[0] // count) + x.shape[1:]), axis=0)


def norm_of(coords):
    wide = coords.astype(jnp.float32)
    return jnp.sum(wide * wide, axis=0)


def squared_dist(left_pts, left_norm, right_pts, right_norm):
    inner = lax.dot_general(
        left_pts, right_pts, (((0,), (0,)), ((), ())), preferred_element_type=jnp.float32
    )
    return left_norm[:, None] + right_norm[None, :] - 2.0 * inner


def shards(points, cells, clone_weight, potential, support_count, cell_count):
    pt_rank = lax.axis_index("pt")
    day_index = lax.axis_index("day")
    day_count = lax.axis_size("day")
    own_pts = points[0]
    per_device = own_pts.shape[1]
    day_pts = lax.all_gather(own_pts, "pt", axis=1, tiled=True)
    support_total = day_pts.shape[1]
    own_weight = clone_weight[0] * potential[0][None, :]
    block_rows = own_weight.shape[0] // lax.axis_size("pt")
    block_weight = swap_blocks(own_weight, 0, 1, (block_rows, day_pts.shape[1]))
    live_total = support_count[0].astype(jnp.float32)
    live_all = (jnp.arange(support_total, dtype=jnp.int32) < support_count[0]).astype(jnp.float32)
    live_own = lax.dynamic_slice_in_dim(live_all, pt_rank * per_device, per_device)
    day_norm = norm_of(day_pts)

    def chain_kernel(source_pts):
        dist = squared_dist(source_pts, norm_of(source_pts), day_pts, day_norm)
        return jnp.exp(-dist).astype(jnp.bfloat16)

    half = day_count // 2
    switch_step = half - 1
    first_forward = day_index < half
    first_route = [(d - 1, d) for d in range(1, half)]
    first_route += [(d + 1, d) for d in range(half, day_count - 1)]
    first_quarter = lax.ppermute(own_pts, "day", first_route)
    first_kernel = chain_kernel(lax.all_gather(first_quarter, "pt", axis=1, tiled=True))

    def settle(values):
        masked = values * live_all[None, :]
        return masked * live_total / jnp.sum(masked, axis=1, keepdims=True)

    rows = jnp.broadcast_to(live_all[None, None, :], (2, block_rows, support_total))
    later_kernel = None
    for step in range(day_count - 1):
        if step == min(1, switch_step):
            later_pts, rows = lax.optimization_barrier((day_pts, rows))
            later_source = jnp.where(
                first_forward,
                lax.ppermute(later_pts, "day", [(d + 1, d) for d in range(half)]),
                lax.ppermute(later_pts, "day", [(d - 1, d) for d in range(half, day_count)]),
            )
        if step == switch_step:
            later_source = lax.optimization_barrier((later_source, rows))[0]
            later_kernel = chain_kernel(later_source)
        kernel = first_kernel if step < switch_step else later_kernel
        forward_from = step
        backward_from = day_count - 1 - step
        sent = (rows * block_weight[None]).astype(jnp.bfloat16)
        outgoing = jnp.where(day_index == forward_from, sent[0], sent[1])
        route = [(forward_from, forward_from + 1), (backward_from, backward_from - 1)]
        incoming = lax.ppermute(outgoing, "day", route)
        fresh = settle(jnp.dot(incoming, kernel, preferred_element_type=jnp.float32))
        keep = jnp.stack([day_index == step + 1, day_index == day_count - 2 - step])
        rows = jnp.where(keep[:, None, None], fresh[None], rows)
    forward_rows = rows[0]
    backward_rows = rows[1]
    both_out = swap_blocks(rows, 2, 1, (2, own_weight.shape[0], per_device))
    forward_out = both_out[0]
    backward_out = both_out[1]
    mass_part = jnp.sum(forward_rows * block_weight * backward_rows, axis=0)
    full_mass = live_all * sum_over_pt(mass_part)
    mass_total = jnp.sum(full_mass)

    cell_total = cell_count[0]
    cell_total_f = cell_total.astype(jnp.float32)
    own_cells = cells[0]
    own_slots = own_cells.shape[1]
    cell_norm = norm_of(own_cells)
    fit_kernel = jnp.exp(-squared_dist(day_pts, day_norm, own_cells, cell_norm))
    density = jnp.sum(full_mass[:, None] * fit_kernel, axis=0) / mass_total
    cell_live = (pt_rank * own_slots + jnp.arange(own_slots, dtype=jnp.int32) < cell_total).astype(
        jnp.float32
    )
    inverse = cell_live / density
    ratio_rows = jnp.sum(fit_kernel * inverse[None, :], axis=1)
    summed = sum_scatter_over_pt(ratio_rows)
    fit_rows_out = live_own / cell_total_f * summed
    return (forward_out[None], backward_out[None], fit_rows_out[None])


def solution(mesh):
    in_specs = (
        P("day", None, "pt"),
        P("day", None, "pt"),
        P("day", None, "pt"),
        P("day", "pt"),
        P("day"),
        P("day"),
    )
    out_specs = (P("day", None, "pt"), P("day", None, "pt"), P("day", "pt"))
    return jax.shard_map(shards, mesh=mesh, in_specs=in_specs, out_specs=out_specs, check_vma=False)
```

```python
import jax
import jax.numpy as jnp
from jax import lax
from jax.sharding import PartitionSpec as P


def shifted(block, axis, distance):
    devices = range(lax.axis_size(axis))
    route = [(i - distance, i) for i in devices if i - distance in devices]
    return lax.ppermute(block, axis, route)


def swap_blocks(x, take_axis, put_axis, put_shape):
    count = lax.axis_size("pt")
    rank = lax.axis_index("pt")
    take = x.shape[take_axis] // count
    put = put_shape[put_axis] // count
    out = jnp.zeros(put_shape, x.dtype)
    for shift in range(count):
        piece = lax.dynamic_slice_in_dim(x, ((rank + shift) % count) * take, take, take_axis)
        if shift:
            piece = lax.ppermute(piece, "pt", [(i, (i + shift) % count) for i in range(count)])
        out = lax.dynamic_update_slice_in_dim(out, piece, ((rank - shift) % count) * put, put_axis)
    return out


def gather_over_pt(x, axis, route=None):
    count = lax.axis_size("pt")
    rank = lax.axis_index("pt")
    shape = list(x.shape)
    shape[axis] *= count
    out = jnp.zeros(shape, x.dtype)
    for shift in range(count):
        if route is None:
            piece = x if shift == 0 else lax.ppermute(
                x, "pt", [((i + shift) % count, i) for i in range(count)]
            )
        else:
            pairs = [
                (src * count + (p + shift) % count, dst * count + p)
                for src, dst in route
                for p in range(count)
            ]
            piece = lax.ppermute(x, ("day", "pt"), pairs)
        out = lax.dynamic_update_slice_in_dim(
            out, piece, ((rank + shift) % count) * x.shape[axis], axis
        )
    return out


def sum_over_pt(x):
    count = lax.axis_size("pt")
    every = swap_blocks(jnp.broadcast_to(x[None], (count,) + x.shape), 0, 0, (count,) + x.shape)
    return jnp.sum(every, axis=0)


def sum_scatter_over_pt(x):
    count = lax.axis_size("pt")
    every = swap_blocks(x, 0, 0, x.shape)
    return jnp.sum(every.reshape((count, x.shape[0] // count) + x.shape[1:]), axis=0)


def norm_of(coords):
    wide = coords.astype(jnp.float32)
    return jnp.sum(wide * wide, axis=0)


def squared_dist(left_pts, left_norm, right_pts, right_norm):
    inner = lax.dot_general(
        left_pts, right_pts, (((0,), (0,)), ((), ())), preferred_element_type=jnp.float32
    )
    return left_norm[:, None] + right_norm[None, :] - 2.0 * inner


def shards(points, cells, clone_weight, potential, support_count, cell_count):
    pt_rank = lax.axis_index("pt")
    day_index = lax.axis_index("day")
    day_count = lax.axis_size("day")
    own_pts = points[0]
    per_device = own_pts.shape[1]
    day_pts = gather_over_pt(own_pts, 1)
    support_total = day_pts.shape[1]
    own_weight = clone_weight[0] * potential[0][None, :]
    block_rows = own_weight.shape[0] // lax.axis_size("pt")
    block_weight = swap_blocks(own_weight, 0, 1, (block_rows, day_pts.shape[1]))
    live_total = support_count[0].astype(jnp.float32)
    live_all = (jnp.arange(support_total, dtype=jnp.int32) < support_count[0]).astype(jnp.float32)
    live_own = lax.dynamic_slice_in_dim(live_all, pt_rank * per_device, per_device)
    day_norm = norm_of(day_pts)

    def chain_kernel(source_pts):
        dist = squared_dist(source_pts, norm_of(source_pts), day_pts, day_norm)
        return jnp.exp(-dist).astype(jnp.bfloat16)

    half = day_count // 2
    switch_step = half - 1
    first_forward = day_index < half
    first_route = [(d - 1, d) for d in range(1, half)]
    first_route += [(d + 1, d) for d in range(half, day_count - 1)]
    first_kernel = chain_kernel(gather_over_pt(own_pts, 1, first_route))

    def settle(values):
        masked = values * live_all[None, :]
        return masked * live_total / jnp.sum(masked, axis=1, keepdims=True)

    rows = jnp.broadcast_to(live_all[None, None, :], (2, block_rows, support_total))
    later_kernel = None
    for step in range(day_count - 1):
        if step == min(1, switch_step):
            later_pts, rows = lax.optimization_barrier((day_pts, rows))
            later_source = jnp.where(
                first_forward,
                lax.ppermute(later_pts, "day", [(d + 1, d) for d in range(half)]),
                lax.ppermute(later_pts, "day", [(d - 1, d) for d in range(half, day_count)]),
            )
        if step == switch_step:
            later_source = lax.optimization_barrier((later_source, rows))[0]
            later_kernel = chain_kernel(later_source)
        kernel = first_kernel if step < switch_step else later_kernel
        forward_from = step
        backward_from = day_count - 1 - step
        sent = (rows * block_weight[None]).astype(jnp.bfloat16)
        outgoing = jnp.where(day_index == forward_from, sent[0], sent[1])
        route = [(forward_from, forward_from + 1), (backward_from, backward_from - 1)]
        incoming = lax.ppermute(outgoing, "day", route)
        fresh = settle(jnp.dot(incoming, kernel, preferred_element_type=jnp.float32))
        keep = jnp.stack([day_index == step + 1, day_index == day_count - 2 - step])
        rows = jnp.where(keep[:, None, None], fresh[None], rows)
    forward_rows = rows[0]
    backward_rows = rows[1]
    both_out = swap_blocks(rows, 2, 1, (2, own_weight.shape[0], per_device))
    forward_out = both_out[0]
    backward_out = both_out[1]
    mass_part = jnp.sum(forward_rows * block_weight * backward_rows, axis=0)
    full_mass = live_all * sum_over_pt(mass_part)
    mass_total = jnp.sum(full_mass)

    cell_total = cell_count[0]
    cell_total_f = cell_total.astype(jnp.float32)
    own_cells = cells[0]
    own_slots = own_cells.shape[1]
    cell_norm = norm_of(own_cells)
    fit_kernel = jnp.exp(-squared_dist(day_pts, day_norm, own_cells, cell_norm))
    density = jnp.sum(full_mass[:, None] * fit_kernel, axis=0) / mass_total
    cell_live = (pt_rank * own_slots + jnp.arange(own_slots, dtype=jnp.int32) < cell_total).astype(
        jnp.float32
    )
    inverse = cell_live / density
    ratio_rows = jnp.sum(fit_kernel * inverse[None, :], axis=1)
    summed = sum_scatter_over_pt(ratio_rows)
    fit_rows_out = live_own / cell_total_f * summed
    return (forward_out[None], backward_out[None], fit_rows_out[None])


def solution(mesh):
    in_specs = (
        P("day", None, "pt"),
        P("day", None, "pt"),
        P("day", None, "pt"),
        P("day", "pt"),
        P("day"),
        P("day"),
    )
    out_specs = (P("day", None, "pt"), P("day", None, "pt"), P("day", "pt"))
    return jax.shard_map(shards, mesh=mesh, in_specs=in_specs, out_specs=out_specs, check_vma=False)
```

```python
import jax
import jax.numpy as jnp
from jax import lax
from jax.sharding import PartitionSpec as P


def shifted(block, axis, distance):
    devices = range(lax.axis_size(axis))
    route = [(i - distance, i) for i in devices if i - distance in devices]
    return lax.ppermute(block, axis, route)


def swap_blocks(x, take_axis, put_axis, put_shape):
    count = lax.axis_size("pt")
    rank = lax.axis_index("pt")
    take = x.shape[take_axis] // count
    put = put_shape[put_axis] // count
    out = jnp.zeros(put_shape, x.dtype)
    for shift in range(count):
        piece = lax.dynamic_slice_in_dim(x, ((rank + shift) % count) * take, take, take_axis)
        if shift:
            piece = lax.ppermute(piece, "pt", [(i, (i + shift) % count) for i in range(count)])
        out = lax.dynamic_update_slice_in_dim(out, piece, ((rank - shift) % count) * put, put_axis)
    return out


def gather_over_pt(x, axis):
    count = lax.axis_size("pt")
    rank = lax.axis_index("pt")
    shape = list(x.shape)
    shape[axis] *= count
    out = jnp.zeros(shape, x.dtype)
    for shift in range(count):
        piece = x if shift == 0 else lax.ppermute(
            x, "pt", [((i + shift) % count, i) for i in range(count)]
        )
        out = lax.dynamic_update_slice_in_dim(
            out, piece, ((rank + shift) % count) * x.shape[axis], axis
        )
    return out


def sum_over_pt(x):
    count = lax.axis_size("pt")
    every = swap_blocks(jnp.broadcast_to(x[None], (count,) + x.shape), 0, 0, (count,) + x.shape)
    return jnp.sum(every, axis=0)


def sum_scatter_over_pt(x):
    count = lax.axis_size("pt")
    every = swap_blocks(x, 0, 0, x.shape)
    return jnp.sum(every.reshape((count, x.shape[0] // count) + x.shape[1:]), axis=0)


def norm_of(coords):
    wide = coords.astype(jnp.float32)
    return jnp.sum(wide * wide, axis=0)


def squared_dist(left_pts, left_norm, right_pts, right_norm):
    inner = lax.dot_general(
        left_pts, right_pts, (((0,), (0,)), ((), ())), preferred_element_type=jnp.float32
    )
    return left_norm[:, None] + right_norm[None, :] - 2.0 * inner


def shards(points, cells, clone_weight, potential, support_count, cell_count):
    pt_rank = lax.axis_index("pt")
    day_index = lax.axis_index("day")
    day_count = lax.axis_size("day")
    own_pts = points[0]
    per_device = own_pts.shape[1]
    day_pts = lax.all_gather(own_pts, "pt", axis=1, tiled=True)
    support_total = day_pts.shape[1]
    own_weight = clone_weight[0] * potential[0][None, :]
    block_rows = own_weight.shape[0] // lax.axis_size("pt")
    block_weight = swap_blocks(own_weight, 0, 1, (block_rows, day_pts.shape[1]))
    live_total = support_count[0].astype(jnp.float32)
    live_all = (jnp.arange(support_total, dtype=jnp.int32) < support_count[0]).astype(jnp.float32)
    live_own = lax.dynamic_slice_in_dim(live_all, pt_rank * per_device, per_device)
    day_norm = norm_of(day_pts)

    def chain_kernel(source_pts):
        dist = squared_dist(source_pts, norm_of(source_pts), day_pts, day_norm)
        return jnp.exp(-dist).astype(jnp.bfloat16)

    half = day_count // 2
    switch_step = half - 1
    first_forward = day_index < half
    first_route = [(d - 1, d) for d in range(1, half)]
    first_route += [(d + 1, d) for d in range(half, day_count - 1)]
    first_quarter = lax.ppermute(own_pts, "day", first_route)
    first_kernel = chain_kernel(gather_over_pt(first_quarter, 1))

    def settle(values):
        masked = values * live_all[None, :]
        return masked * live_total / jnp.sum(masked, axis=1, keepdims=True)

    rows = jnp.broadcast_to(live_all[None, None, :], (2, block_rows, support_total))
    later_kernel = None
    for step in range(day_count - 1):
        if step == min(1, switch_step):
            later_pts, rows = lax.optimization_barrier((day_pts, rows))
            later_source = jnp.where(
                first_forward,
                lax.ppermute(later_pts, "day", [(d + 1, d) for d in range(half)]),
                lax.ppermute(later_pts, "day", [(d - 1, d) for d in range(half, day_count)]),
            )
        if step == switch_step:
            later_source = lax.optimization_barrier((later_source, rows))[0]
            later_kernel = chain_kernel(later_source)
        kernel = first_kernel if step < switch_step else later_kernel
        forward_from = step
        backward_from = day_count - 1 - step
        sent = (rows * block_weight[None]).astype(jnp.bfloat16)
        outgoing = jnp.where(day_index == forward_from, sent[0], sent[1])
        route = [(forward_from, forward_from + 1), (backward_from, backward_from - 1)]
        incoming = lax.ppermute(outgoing, "day", route)
        fresh = settle(jnp.dot(incoming, kernel, preferred_element_type=jnp.float32))
        keep = jnp.stack([day_index == step + 1, day_index == day_count - 2 - step])
        rows = jnp.where(keep[:, None, None], fresh[None], rows)
    forward_rows = rows[0]
    backward_rows = rows[1]
    both_out = swap_blocks(rows, 2, 1, (2, own_weight.shape[0], per_device))
    forward_out = both_out[0]
    backward_out = both_out[1]
    mass_part = jnp.sum(forward_rows * block_weight * backward_rows, axis=0)
    full_mass = live_all * sum_over_pt(mass_part)
    mass_total = jnp.sum(full_mass)

    cell_total = cell_count[0]
    cell_total_f = cell_total.astype(jnp.float32)
    own_cells = cells[0]
    own_slots = own_cells.shape[1]
    cell_norm = norm_of(own_cells)
    fit_kernel = jnp.exp(-squared_dist(day_pts, day_norm, own_cells, cell_norm))
    density = jnp.sum(full_mass[:, None] * fit_kernel, axis=0) / mass_total
    cell_live = (pt_rank * own_slots + jnp.arange(own_slots, dtype=jnp.int32) < cell_total).astype(
        jnp.float32
    )
    inverse = cell_live / density
    ratio_rows = jnp.sum(fit_kernel * inverse[None, :], axis=1)
    summed = sum_scatter_over_pt(ratio_rows)
    fit_rows_out = live_own / cell_total_f * summed
    return (forward_out[None], backward_out[None], fit_rows_out[None])


def solution(mesh):
    in_specs = (
        P("day", None, "pt"),
        P("day", None, "pt"),
        P("day", None, "pt"),
        P("day", "pt"),
        P("day"),
        P("day"),
    )
    out_specs = (P("day", None, "pt"), P("day", None, "pt"), P("day", "pt"))
    return jax.shard_map(shards, mesh=mesh, in_specs=in_specs, out_specs=out_specs, check_vma=False)
```

```python
import jax
import jax.numpy as jnp
from jax import lax
from jax.sharding import PartitionSpec as P


def shifted(block, axis, distance):
    devices = range(lax.axis_size(axis))
    route = [(i - distance, i) for i in devices if i - distance in devices]
    return lax.ppermute(block, axis, route)


def swap_blocks(x, take_axis, put_axis, put_shape):
    count = lax.axis_size("pt")
    rank = lax.axis_index("pt")
    take = x.shape[take_axis] // count
    put = put_shape[put_axis] // count
    out = jnp.zeros(put_shape, x.dtype)
    for shift in range(count):
        piece = lax.dynamic_slice_in_dim(x, ((rank + shift) % count) * take, take, take_axis)
        if shift:
            piece = lax.ppermute(piece, "pt", [(i, (i + shift) % count) for i in range(count)])
        out = lax.dynamic_update_slice_in_dim(out, piece, ((rank - shift) % count) * put, put_axis)
    return out


def gather_over_pt(x, axis):
    count = lax.axis_size("pt")
    rank = lax.axis_index("pt")
    shape = list(x.shape)
    shape[axis] *= count
    out = jnp.zeros(shape, x.dtype)
    for shift in range(count):
        piece = x if shift == 0 else lax.ppermute(
            x, "pt", [((i + shift) % count, i) for i in range(count)]
        )
        out = lax.dynamic_update_slice_in_dim(
            out, piece, ((rank + shift) % count) * x.shape[axis], axis
        )
    return out


def sum_over_pt(x):
    count = lax.axis_size("pt")
    every = swap_blocks(jnp.broadcast_to(x[None], (count,) + x.shape), 0, 0, (count,) + x.shape)
    return jnp.sum(every, axis=0)


def sum_scatter_over_pt(x):
    count = lax.axis_size("pt")
    every = swap_blocks(x, 0, 0, x.shape)
    return jnp.sum(every.reshape((count, x.shape[0] // count) + x.shape[1:]), axis=0)


def norm_of(coords):
    wide = coords.astype(jnp.float32)
    return jnp.sum(wide * wide, axis=0)


def squared_dist(left_pts, left_norm, right_pts, right_norm):
    inner = lax.dot_general(
        left_pts, right_pts, (((0,), (0,)), ((), ())), preferred_element_type=jnp.float32
    )
    return left_norm[:, None] + right_norm[None, :] - 2.0 * inner


def shards(points, cells, clone_weight, potential, support_count, cell_count):
    pt_rank = lax.axis_index("pt")
    day_index = lax.axis_index("day")
    day_count = lax.axis_size("day")
    own_pts = points[0]
    per_device = own_pts.shape[1]
    day_pts = lax.all_gather(own_pts, "pt", axis=1, tiled=True)
    support_total = day_pts.shape[1]
    own_weight = clone_weight[0] * potential[0][None, :]
    block_rows = own_weight.shape[0] // lax.axis_size("pt")
    block_weight = swap_blocks(own_weight, 0, 1, (block_rows, day_pts.shape[1]))
    live_total = support_count[0].astype(jnp.float32)
    live_all = (jnp.arange(support_total, dtype=jnp.int32) < support_count[0]).astype(jnp.float32)
    live_own = lax.dynamic_slice_in_dim(live_all, pt_rank * per_device, per_device)
    day_norm = norm_of(day_pts)

    def chain_kernel(source_pts):
        dist = squared_dist(source_pts, norm_of(source_pts), day_pts, day_norm)
        return jnp.exp(-dist).astype(jnp.bfloat16)

    half = day_count // 2
    switch_step = half - 1
    first_forward = day_index < half
    first_route = [(d - 1, d) for d in range(1, half)]
    first_route += [(d + 1, d) for d in range(half, day_count - 1)]
    first_quarter = lax.ppermute(own_pts, "day", first_route)
    first_kernel = chain_kernel(gather_over_pt(first_quarter, 1))

    def settle(values):
        masked = values * live_all[None, :]
        return masked * live_total / jnp.sum(masked, axis=1, keepdims=True)

    rows = jnp.broadcast_to(live_all[None, None, :], (2, block_rows, support_total))
    later_kernel = None
    for step in range(day_count - 1):
        if step == min(1, switch_step):
            later_pts, rows = lax.optimization_barrier((day_pts, rows))
            later_source = jnp.where(
                first_forward,
                lax.ppermute(later_pts, "day", [(d + 1, d) for d in range(half)]),
                lax.ppermute(later_pts, "day", [(d - 1, d) for d in range(half, day_count)]),
            )
        if step == switch_step:
            later_source = lax.optimization_barrier((later_source, rows))[0]
            later_kernel = chain_kernel(later_source)
        kernel = first_kernel if step < switch_step else later_kernel
        forward_from = step
        backward_from = day_count - 1 - step
        sent = (rows * block_weight[None]).astype(jnp.bfloat16)
        outgoing = jnp.where(day_index == forward_from, sent[0], sent[1])
        route = [(forward_from, forward_from + 1), (backward_from, backward_from - 1)]
        incoming = lax.ppermute(outgoing, "day", route)
        fresh = settle(jnp.dot(incoming, kernel, preferred_element_type=jnp.float32))
        keep = jnp.stack([day_index == step + 1, day_index == day_count - 2 - step])
        rows = jnp.where(keep[:, None, None], fresh[None], rows)
    forward_rows = rows[0]
    backward_rows = rows[1]
    mass_part = jnp.sum(forward_rows * block_weight * backward_rows, axis=0)
    pt_count = lax.axis_size("pt")
    mass_rows = mass_part.reshape(pt_count, per_device)
    both_out = jnp.zeros((2 * pt_count, block_rows, per_device), jnp.float32)
    every_mass = jnp.zeros((pt_count, support_total), jnp.float32)
    for shift in range(pt_count):
        block = lax.dynamic_slice_in_dim(rows, ((pt_rank + shift) % pt_count) * per_device, per_device, 2)
        packed = jnp.concatenate([block.reshape(2 * block_rows, per_device), mass_rows], axis=0)
        if shift:
            packed = lax.ppermute(
                packed, "pt", [(i, (i + shift) % pt_count) for i in range(pt_count)]
            )
        origin = (pt_rank - shift) % pt_count
        piece = packed[: 2 * block_rows].reshape(2, 1, block_rows, per_device)
        both_out = lax.dynamic_update_slice_in_dim(
            both_out.reshape(2, pt_count, block_rows, per_device), piece, origin, 1
        ).reshape(2 * pt_count, block_rows, per_device)
        every_mass = lax.dynamic_update_slice_in_dim(
            every_mass, packed[2 * block_rows:].reshape(1, support_total), origin, 0
        )
    both_out = both_out.reshape(2, pt_count * block_rows, per_device)
    forward_out = both_out[0]
    backward_out = both_out[1]
    full_mass = live_all * jnp.sum(every_mass, axis=0)
    mass_total = jnp.sum(full_mass)

    cell_total = cell_count[0]
    cell_total_f = cell_total.astype(jnp.float32)
    own_cells = cells[0]
    own_slots = own_cells.shape[1]
    cell_norm = norm_of(own_cells)
    fit_kernel = jnp.exp(-squared_dist(day_pts, day_norm, own_cells, cell_norm))
    density = jnp.sum(full_mass[:, None] * fit_kernel, axis=0) / mass_total
    cell_live = (pt_rank * own_slots + jnp.arange(own_slots, dtype=jnp.int32) < cell_total).astype(
        jnp.float32
    )
    inverse = cell_live / density
    ratio_rows = jnp.sum(fit_kernel * inverse[None, :], axis=1)
    summed = sum_scatter_over_pt(ratio_rows)
    fit_rows_out = live_own / cell_total_f * summed
    return (forward_out[None], backward_out[None], fit_rows_out[None])


def solution(mesh):
    in_specs = (
        P("day", None, "pt"),
        P("day", None, "pt"),
        P("day", None, "pt"),
        P("day", "pt"),
        P("day"),
        P("day"),
    )
    out_specs = (P("day", None, "pt"), P("day", None, "pt"), P("day", "pt"))
    return jax.shard_map(shards, mesh=mesh, in_specs=in_specs, out_specs=out_specs, check_vma=False)
```

```python
import jax
import jax.numpy as jnp
from jax import lax
from jax.sharding import PartitionSpec as P


def shifted(block, axis, distance):
    devices = range(lax.axis_size(axis))
    route = [(i - distance, i) for i in devices if i - distance in devices]
    return lax.ppermute(block, axis, route)


def swap_blocks(x, take_axis, put_axis, put_shape):
    count = lax.axis_size("pt")
    rank = lax.axis_index("pt")
    take = x.shape[take_axis] // count
    put = put_shape[put_axis] // count
    out = jnp.zeros(put_shape, x.dtype)
    for shift in range(count):
        piece = lax.dynamic_slice_in_dim(x, ((rank + shift) % count) * take, take, take_axis)
        if shift:
            piece = lax.ppermute(piece, "pt", [(i, (i + shift) % count) for i in range(count)])
        out = lax.dynamic_update_slice_in_dim(out, piece, ((rank - shift) % count) * put, put_axis)
    return out


def sum_over_pt(x):
    count = lax.axis_size("pt")
    every = swap_blocks(jnp.broadcast_to(x[None], (count,) + x.shape), 0, 0, (count,) + x.shape)
    return jnp.sum(every, axis=0)


def sum_scatter_over_pt(x):
    count = lax.axis_size("pt")
    every = swap_blocks(x, 0, 0, x.shape)
    return jnp.sum(every.reshape((count, x.shape[0] // count) + x.shape[1:]), axis=0)


def norm_of(coords):
    wide = coords.astype(jnp.float32)
    return jnp.sum(wide * wide, axis=0)


def squared_dist(left_pts, left_norm, right_pts, right_norm):
    inner = lax.dot_general(
        left_pts, right_pts, (((0,), (0,)), ((), ())), preferred_element_type=jnp.float32
    )
    return left_norm[:, None] + right_norm[None, :] - 2.0 * inner


def shards(points, cells, clone_weight, potential, support_count, cell_count):
    pt_rank = lax.axis_index("pt")
    day_index = lax.axis_index("day")
    day_count = lax.axis_size("day")
    own_pts = points[0]
    per_device = own_pts.shape[1]
    day_pts = lax.all_gather(own_pts, "pt", axis=1, tiled=True)
    support_total = day_pts.shape[1]
    own_weight = clone_weight[0] * potential[0][None, :]
    block_rows = own_weight.shape[0] // lax.axis_size("pt")
    block_weight = swap_blocks(own_weight, 0, 1, (block_rows, day_pts.shape[1]))
    live_total = support_count[0].astype(jnp.float32)
    live_all = (jnp.arange(support_total, dtype=jnp.int32) < support_count[0]).astype(jnp.float32)
    live_own = lax.dynamic_slice_in_dim(live_all, pt_rank * per_device, per_device)
    day_norm = norm_of(day_pts)

    def chain_kernel(source_pts):
        dist = squared_dist(source_pts, norm_of(source_pts), day_pts, day_norm)
        return jnp.exp(-dist).astype(jnp.bfloat16)

    half = day_count // 2
    switch_step = half - 1
    first_forward = day_index < half
    first_route = [(d - 1, d) for d in range(1, half)]
    first_route += [(d + 1, d) for d in range(half, day_count - 1)]
    first_kernel = chain_kernel(lax.ppermute(day_pts, "day", first_route))

    def settle(values):
        masked = values * live_all[None, :]
        return masked * live_total / jnp.sum(masked, axis=1, keepdims=True)

    rows = jnp.broadcast_to(live_all[None, None, :], (2, block_rows, support_total))
    later_kernel = None
    for step in range(day_count - 1):
        if step == min(1, switch_step):
            later_pts = lax.optimization_barrier((day_pts, rows))[0]
            later_source = jnp.where(
                first_forward,
                lax.ppermute(later_pts, "day", [(d + 1, d) for d in range(half)]),
                lax.ppermute(later_pts, "day", [(d - 1, d) for d in range(half, day_count)]),
            )
        if step == switch_step:
            later_source = lax.optimization_barrier((later_source, rows))[0]
            later_kernel = chain_kernel(later_source)
        kernel = first_kernel if step < switch_step else later_kernel
        forward_from = step
        backward_from = day_count - 1 - step
        sent = (rows * block_weight[None]).astype(jnp.bfloat16)
        outgoing = jnp.where(day_index == forward_from, sent[0], sent[1])
        route = [(forward_from, forward_from + 1), (backward_from, backward_from - 1)]
        incoming = lax.ppermute(outgoing, "day", route)
        fresh = settle(jnp.dot(incoming, kernel, preferred_element_type=jnp.float32))
        keep = jnp.stack([day_index == step + 1, day_index == day_count - 2 - step])
        rows = jnp.where(keep[:, None, None], fresh[None], rows)
    forward_rows = rows[0]
    backward_rows = rows[1]
    both_out = swap_blocks(rows, 2, 1, (2, own_weight.shape[0], per_device))
    forward_out = both_out[0]
    backward_out = both_out[1]
    mass_part = jnp.sum(forward_rows * block_weight * backward_rows, axis=0)
    full_mass = live_all * sum_over_pt(mass_part)
    mass_total = jnp.sum(full_mass)

    cell_total = cell_count[0]
    cell_total_f = cell_total.astype(jnp.float32)
    own_cells = cells[0]
    own_slots = own_cells.shape[1]
    cell_norm = norm_of(own_cells)
    fit_kernel = jnp.exp(-squared_dist(own_cells, cell_norm, day_pts, day_norm))
    density = jnp.sum(fit_kernel * full_mass[None, :], axis=1) / mass_total
    cell_live = (pt_rank * own_slots + jnp.arange(own_slots, dtype=jnp.int32) < cell_total).astype(
        jnp.float32
    )
    inverse = cell_live / density
    ratio_rows = jnp.sum(fit_kernel * inverse[:, None], axis=0)
    summed = sum_scatter_over_pt(ratio_rows)
    fit_rows_out = live_own / cell_total_f * summed
    return (forward_out[None], backward_out[None], fit_rows_out[None])


def solution(mesh):
    in_specs = (
        P("day", None, "pt"),
        P("day", None, "pt"),
        P("day", None, "pt"),
        P("day", "pt"),
        P("day"),
        P("day"),
    )
    out_specs = (P("day", None, "pt"), P("day", None, "pt"), P("day", "pt"))
    return jax.shard_map(shards, mesh=mesh, in_specs=in_specs, out_specs=out_specs, check_vma=False)
```

```python
import jax
import jax.numpy as jnp
from jax import lax
from jax.sharding import PartitionSpec as P


def shifted(block, axis, distance):
    devices = range(lax.axis_size(axis))
    route = [(i - distance, i) for i in devices if i - distance in devices]
    return lax.ppermute(block, axis, route)


def swap_blocks(x, take_axis, put_axis, put_shape):
    count = lax.axis_size("pt")
    rank = lax.axis_index("pt")
    take = x.shape[take_axis] // count
    put = put_shape[put_axis] // count
    out = jnp.zeros(put_shape, x.dtype)
    for shift in range(count):
        piece = lax.dynamic_slice_in_dim(x, ((rank + shift) % count) * take, take, take_axis)
        if shift:
            piece = lax.ppermute(piece, "pt", [(i, (i + shift) % count) for i in range(count)])
        out = lax.dynamic_update_slice_in_dim(out, piece, ((rank - shift) % count) * put, put_axis)
    return out


def sum_over_pt(x):
    count = lax.axis_size("pt")
    every = swap_blocks(jnp.broadcast_to(x[None], (count,) + x.shape), 0, 0, (count,) + x.shape)
    return jnp.sum(every, axis=0)


def sum_scatter_over_pt(x):
    count = lax.axis_size("pt")
    every = swap_blocks(x, 0, 0, x.shape)
    return jnp.sum(every.reshape((count, x.shape[0] // count) + x.shape[1:]), axis=0)


def norm_of(coords):
    wide = coords.astype(jnp.float32)
    return jnp.sum(wide * wide, axis=0)


def squared_dist(left_pts, left_norm, right_pts, right_norm):
    inner = lax.dot_general(
        left_pts, right_pts, (((0,), (0,)), ((), ())), preferred_element_type=jnp.float32
    )
    return left_norm[:, None] + right_norm[None, :] - 2.0 * inner


def shards(points, cells, clone_weight, potential, support_count, cell_count):
    pt_rank = lax.axis_index("pt")
    day_index = lax.axis_index("day")
    day_count = lax.axis_size("day")
    own_pts = points[0]
    per_device = own_pts.shape[1]
    day_pts = lax.all_gather(own_pts, "pt", axis=1, tiled=True)
    support_total = day_pts.shape[1]
    own_weight = clone_weight[0] * potential[0][None, :]
    block_rows = own_weight.shape[0] // lax.axis_size("pt")
    block_weight = swap_blocks(own_weight, 0, 1, (block_rows, day_pts.shape[1]))
    live_total = support_count[0].astype(jnp.float32)
    live_all = (jnp.arange(support_total, dtype=jnp.int32) < support_count[0]).astype(jnp.float32)
    live_own = lax.dynamic_slice_in_dim(live_all, pt_rank * per_device, per_device)
    day_norm = norm_of(day_pts)

    def chain_kernel(source_pts):
        dist = squared_dist(source_pts, norm_of(source_pts), day_pts, day_norm)
        return jnp.exp(-dist).astype(jnp.bfloat16)

    half = day_count // 2
    even_day = day_index % 2 == 0
    pair_route = [(d + 1, d) if d % 2 == 0 else (d - 1, d) for d in range(day_count)]
    link_route = [(d - 1, d) if d % 2 == 0 else (d + 1, d) for d in range(1, day_count - 1)]
    other_kernel = chain_kernel(lax.ppermute(day_pts, "day", pair_route))
    other_weight = lax.ppermute(block_weight, "day", pair_route)
    other_count = lax.ppermute(support_count, "day", pair_route)[0]
    other_total = other_count.astype(jnp.float32)
    other_live = (jnp.arange(support_total, dtype=jnp.int32) < other_count).astype(jnp.float32)
    link_pts = lax.ppermute(day_pts, "day", link_route)

    def settle(values, live, total):
        masked = values * live[None, :]
        return masked * total / jnp.sum(masked, axis=1, keepdims=True)

    seed_rows = jnp.broadcast_to(live_all[None, :], (block_rows, support_total))
    own_rows = seed_rows
    handed_rows = jnp.zeros_like(seed_rows)
    incoming = None
    link_kernel = None
    for round_index in range(half):
        forward_day = 2 * round_index
        backward_day = day_count - 1 - 2 * round_index
        if round_index == 0:
            current = seed_rows
        else:
            current = settle(
                jnp.dot(incoming, link_kernel, preferred_element_type=jnp.float32),
                live_all,
                live_total,
            )
            active = (day_index == forward_day) | (day_index == backward_day)
            own_rows = jnp.where(active, current, own_rows)
        sent = (current * block_weight).astype(jnp.bfloat16)
        following = settle(
            lax.dot_general(
                sent, other_kernel, (((1,), (1,)), ((), ())), preferred_element_type=jnp.float32
            ),
            other_live,
            other_total,
        )
        if round_index == 0:
            link_pts = lax.optimization_barrier((link_pts, following))[0]
            link_kernel = chain_kernel(link_pts)
        if round_index < half - 1:
            outgoing = (following * other_weight).astype(jnp.bfloat16)
            incoming = lax.ppermute(
                outgoing, "day", [(forward_day, forward_day + 2), (backward_day, backward_day - 2)]
            )
        handed = lax.ppermute(
            following, "day", [(forward_day, forward_day + 1), (backward_day, backward_day - 1)]
        )
        receiver = (day_index == forward_day + 1) | (day_index == backward_day - 1)
        handed_rows = jnp.where(receiver, handed, handed_rows)
    rows = jnp.stack(
        [
            jnp.where(even_day, own_rows, handed_rows),
            jnp.where(even_day, handed_rows, own_rows),
        ]
    )
    forward_rows = rows[0]
    backward_rows = rows[1]
    both_out = swap_blocks(rows, 2, 1, (2, own_weight.shape[0], per_device))
    forward_out = both_out[0]
    backward_out = both_out[1]
    mass_part = jnp.sum(forward_rows * block_weight * backward_rows, axis=0)
    full_mass = live_all * sum_over_pt(mass_part)
    mass_total = jnp.sum(full_mass)

    cell_total = cell_count[0]
    cell_total_f = cell_total.astype(jnp.float32)
    own_cells = cells[0]
    own_slots = own_cells.shape[1]
    cell_norm = norm_of(own_cells)
    fit_kernel = jnp.exp(-squared_dist(day_pts, day_norm, own_cells, cell_norm))
    density = jnp.sum(full_mass[:, None] * fit_kernel, axis=0) / mass_total
    cell_live = (pt_rank * own_slots + jnp.arange(own_slots, dtype=jnp.int32) < cell_total).astype(
        jnp.float32
    )
    inverse = cell_live / density
    ratio_rows = jnp.sum(fit_kernel * inverse[None, :], axis=1)
    summed = sum_scatter_over_pt(ratio_rows)
    fit_rows_out = live_own / cell_total_f * summed
    return (forward_out[None], backward_out[None], fit_rows_out[None])


def solution(mesh):
    in_specs = (
        P("day", None, "pt"),
        P("day", None, "pt"),
        P("day", None, "pt"),
        P("day", "pt"),
        P("day"),
        P("day"),
    )
    out_specs = (P("day", None, "pt"), P("day", None, "pt"), P("day", "pt"))
    return jax.shard_map(shards, mesh=mesh, in_specs=in_specs, out_specs=out_specs, check_vma=False)
```

```python
import jax
import jax.numpy as jnp
from jax import lax
from jax.sharding import PartitionSpec as P


def shifted(block, axis, distance):
    devices = range(lax.axis_size(axis))
    route = [(i - distance, i) for i in devices if i - distance in devices]
    return lax.ppermute(block, axis, route)


def swap_blocks(x, take_axis, put_axis, put_shape):
    count = lax.axis_size("pt")
    rank = lax.axis_index("pt")
    take = x.shape[take_axis] // count
    put = put_shape[put_axis] // count
    out = jnp.zeros(put_shape, x.dtype)
    for shift in range(count):
        piece = lax.dynamic_slice_in_dim(x, ((rank + shift) % count) * take, take, take_axis)
        if shift:
            piece = lax.ppermute(piece, "pt", [(i, (i + shift) % count) for i in range(count)])
        out = lax.dynamic_update_slice_in_dim(out, piece, ((rank - shift) % count) * put, put_axis)
    return out


def sum_over_pt(x):
    count = lax.axis_size("pt")
    every = swap_blocks(jnp.broadcast_to(x[None], (count,) + x.shape), 0, 0, (count,) + x.shape)
    return jnp.sum(every, axis=0)


def sum_scatter_over_pt(x):
    count = lax.axis_size("pt")
    every = swap_blocks(x, 0, 0, x.shape)
    return jnp.sum(every.reshape((count, x.shape[0] // count) + x.shape[1:]), axis=0)


def norm_of(coords):
    wide = coords.astype(jnp.float32)
    return jnp.sum(wide * wide, axis=0)


def squared_dist(left_pts, left_norm, right_pts, right_norm):
    inner = lax.dot_general(
        left_pts, right_pts, (((0,), (0,)), ((), ())), preferred_element_type=jnp.float32
    )
    return left_norm[:, None] + right_norm[None, :] - 2.0 * inner


def shards(points, cells, clone_weight, potential, support_count, cell_count):
    pt_rank = lax.axis_index("pt")
    day_index = lax.axis_index("day")
    day_count = lax.axis_size("day")
    own_pts = points[0]
    per_device = own_pts.shape[1]
    day_pts = lax.all_gather(own_pts, "pt", axis=1, tiled=True)
    support_total = day_pts.shape[1]
    own_weight = clone_weight[0] * potential[0][None, :]
    block_rows = own_weight.shape[0] // lax.axis_size("pt")
    block_weight = swap_blocks(own_weight, 0, 1, (block_rows, day_pts.shape[1]))
    live_total = support_count[0].astype(jnp.float32)
    live_all = (jnp.arange(support_total, dtype=jnp.int32) < support_count[0]).astype(jnp.float32)
    live_own = lax.dynamic_slice_in_dim(live_all, pt_rank * per_device, per_device)
    day_norm = norm_of(day_pts)

    def chain_kernel(source_pts):
        dist = squared_dist(source_pts, norm_of(source_pts), day_pts, day_norm)
        return jnp.exp(-dist).astype(jnp.bfloat16)

    half = day_count // 2
    even_day = day_index % 2 == 0
    pair_route = [(d + 1, d) if d % 2 == 0 else (d - 1, d) for d in range(day_count)]
    link_route = [(d - 1, d) if d % 2 == 0 else (d + 1, d) for d in range(1, day_count - 1)]
    other_pts = lax.ppermute(day_pts, "day", pair_route)
    other_kernel = jnp.exp(
        -squared_dist(day_pts, day_norm, other_pts, norm_of(other_pts))
    ).astype(jnp.bfloat16)
    other_weight = lax.ppermute(block_weight, "day", pair_route)
    other_count = lax.ppermute(support_count, "day", pair_route)[0]
    other_total = other_count.astype(jnp.float32)
    other_live = (jnp.arange(support_total, dtype=jnp.int32) < other_count).astype(jnp.float32)
    link_pts = lax.ppermute(day_pts, "day", link_route)

    def settle(values, live, total):
        masked = values * live[None, :]
        return masked * total / jnp.sum(masked, axis=1, keepdims=True)

    seed_rows = jnp.broadcast_to(live_all[None, :], (block_rows, support_total))
    own_rows = seed_rows
    handed_rows = jnp.zeros_like(seed_rows)
    incoming = None
    link_kernel = None
    for round_index in range(half):
        forward_day = 2 * round_index
        backward_day = day_count - 1 - 2 * round_index
        if round_index == 0:
            current = seed_rows
        else:
            current = settle(
                jnp.dot(incoming, link_kernel, preferred_element_type=jnp.float32),
                live_all,
                live_total,
            )
            active = (day_index == forward_day) | (day_index == backward_day)
            own_rows = jnp.where(active, current, own_rows)
        sent = (current * block_weight).astype(jnp.bfloat16)
        following = settle(
            jnp.dot(sent, other_kernel, preferred_element_type=jnp.float32),
            other_live,
            other_total,
        )
        if round_index == 0:
            link_pts = lax.optimization_barrier((link_pts, following))[0]
            link_kernel = chain_kernel(link_pts)
        if round_index < half - 1:
            outgoing = (following * other_weight).astype(jnp.bfloat16)
            incoming = lax.ppermute(
                outgoing, "day", [(forward_day, forward_day + 2), (backward_day, backward_day - 2)]
            )
        handed = lax.ppermute(
            following, "day", [(forward_day, forward_day + 1), (backward_day, backward_day - 1)]
        )
        receiver = (day_index == forward_day + 1) | (day_index == backward_day - 1)
        handed_rows = jnp.where(receiver, handed, handed_rows)
    rows = jnp.stack(
        [
            jnp.where(even_day, own_rows, handed_rows),
            jnp.where(even_day, handed_rows, own_rows),
        ]
    )
    forward_rows = rows[0]
    backward_rows = rows[1]
    both_out = swap_blocks(rows, 2, 1, (2, own_weight.shape[0], per_device))
    forward_out = both_out[0]
    backward_out = both_out[1]
    mass_part = jnp.sum(forward_rows * block_weight * backward_rows, axis=0)
    full_mass = live_all * sum_over_pt(mass_part)
    mass_total = jnp.sum(full_mass)

    cell_total = cell_count[0]
    cell_total_f = cell_total.astype(jnp.float32)
    own_cells = cells[0]
    own_slots = own_cells.shape[1]
    cell_norm = norm_of(own_cells)
    fit_kernel = jnp.exp(-squared_dist(day_pts, day_norm, own_cells, cell_norm))
    density = jnp.sum(full_mass[:, None] * fit_kernel, axis=0) / mass_total
    cell_live = (pt_rank * own_slots + jnp.arange(own_slots, dtype=jnp.int32) < cell_total).astype(
        jnp.float32
    )
    inverse = cell_live / density
    ratio_rows = jnp.sum(fit_kernel * inverse[None, :], axis=1)
    summed = sum_scatter_over_pt(ratio_rows)
    fit_rows_out = live_own / cell_total_f * summed
    return (forward_out[None], backward_out[None], fit_rows_out[None])


def solution(mesh):
    in_specs = (
        P("day", None, "pt"),
        P("day", None, "pt"),
        P("day", None, "pt"),
        P("day", "pt"),
        P("day"),
        P("day"),
    )
    out_specs = (P("day", None, "pt"), P("day", None, "pt"), P("day", "pt"))
    return jax.shard_map(shards, mesh=mesh, in_specs=in_specs, out_specs=out_specs, check_vma=False)
```

```python
import jax
import jax.numpy as jnp
from jax import lax
from jax.sharding import PartitionSpec as P


def shifted(block, axis, distance):
    devices = range(lax.axis_size(axis))
    route = [(i - distance, i) for i in devices if i - distance in devices]
    return lax.ppermute(block, axis, route)


def swap_blocks(x, take_axis, put_axis, put_shape):
    count = lax.axis_size("pt")
    rank = lax.axis_index("pt")
    take = x.shape[take_axis] // count
    put = put_shape[put_axis] // count
    out = jnp.zeros(put_shape, x.dtype)
    for shift in range(count):
        piece = lax.dynamic_slice_in_dim(x, ((rank + shift) % count) * take, take, take_axis)
        if shift:
            piece = lax.ppermute(piece, "pt", [(i, (i + shift) % count) for i in range(count)])
        out = lax.dynamic_update_slice_in_dim(out, piece, ((rank - shift) % count) * put, put_axis)
    return out


def sum_over_pt(x):
    count = lax.axis_size("pt")
    every = swap_blocks(jnp.broadcast_to(x[None], (count,) + x.shape), 0, 0, (count,) + x.shape)
    return jnp.sum(every, axis=0)


def sum_scatter_over_pt(x):
    count = lax.axis_size("pt")
    every = swap_blocks(x, 0, 0, x.shape)
    return jnp.sum(every.reshape((count, x.shape[0] // count) + x.shape[1:]), axis=0)


def norm_of(coords):
    wide = coords.astype(jnp.float32)
    return jnp.sum(wide * wide, axis=0)


def squared_dist(left_pts, left_norm, right_pts, right_norm):
    inner = lax.dot_general(
        left_pts, right_pts, (((0,), (0,)), ((), ())), preferred_element_type=jnp.float32
    )
    return left_norm[:, None] + right_norm[None, :] - 2.0 * inner


def shards(points, cells, clone_weight, potential, support_count, cell_count):
    pt_rank = lax.axis_index("pt")
    day_index = lax.axis_index("day")
    day_count = lax.axis_size("day")
    own_pts = points[0]
    per_device = own_pts.shape[1]
    day_pts = lax.all_gather(own_pts, "pt", axis=1, tiled=True)
    support_total = day_pts.shape[1]
    own_weight = clone_weight[0] * potential[0][None, :]
    block_rows = own_weight.shape[0] // lax.axis_size("pt")
    block_weight = swap_blocks(own_weight, 0, 1, (block_rows, day_pts.shape[1]))
    live_total = support_count[0].astype(jnp.float32)
    live_all = (jnp.arange(support_total, dtype=jnp.int32) < support_count[0]).astype(jnp.float32)
    live_own = lax.dynamic_slice_in_dim(live_all, pt_rank * per_device, per_device)
    day_norm = norm_of(day_pts)

    def chain_kernel(source_pts):
        dist = squared_dist(source_pts, norm_of(source_pts), day_pts, day_norm)
        return jnp.exp(-dist).astype(jnp.bfloat16)

    half = day_count // 2
    even_day = day_index % 2 == 0
    pair_route = [(d + 1, d) if d % 2 == 0 else (d - 1, d) for d in range(day_count)]
    link_route = [(d - 1, d) if d % 2 == 0 else (d + 1, d) for d in range(1, day_count - 1)]
    other_pts = lax.ppermute(day_pts, "day", pair_route)
    other_kernel = jnp.exp(
        -squared_dist(day_pts, day_norm, other_pts, norm_of(other_pts))
    ).astype(jnp.bfloat16)
    other_weight = lax.ppermute(block_weight, "day", pair_route)
    other_count = lax.ppermute(support_count, "day", pair_route)[0]
    other_total = other_count.astype(jnp.float32)
    other_live = (jnp.arange(support_total, dtype=jnp.int32) < other_count).astype(jnp.float32)
    link_pts = lax.ppermute(day_pts, "day", link_route)

    def settle(values, live, total):
        masked = values * live[None, :]
        return masked * total / jnp.sum(masked, axis=1, keepdims=True)

    seed_rows = jnp.broadcast_to(live_all[None, :], (block_rows, support_total))
    own_rows = seed_rows
    handed_rows = jnp.zeros_like(seed_rows)
    incoming = None
    link_kernel = None
    for round_index in range(half):
        forward_day = 2 * round_index
        backward_day = day_count - 1 - 2 * round_index
        if round_index == 0:
            current = seed_rows
        else:
            current = settle(
                jnp.dot(incoming, link_kernel, preferred_element_type=jnp.float32),
                live_all,
                live_total,
            )
            active = (day_index == forward_day) | (day_index == backward_day)
            own_rows = jnp.where(active, current, own_rows)
        sent = (current * block_weight).astype(jnp.bfloat16)
        following = settle(
            jnp.dot(sent, other_kernel, preferred_element_type=jnp.float32),
            other_live,
            other_total,
        )
        if round_index == 0:
            link_pts = lax.optimization_barrier((link_pts, following))[0]
            link_kernel = chain_kernel(link_pts)
        if round_index < half - 1:
            outgoing = (following * other_weight).astype(jnp.bfloat16)
            incoming = lax.ppermute(
                outgoing, "day", [(forward_day, forward_day + 2), (backward_day, backward_day - 2)]
            )
        handed = lax.ppermute(
            following, "day", [(forward_day, forward_day + 1), (backward_day, backward_day - 1)]
        )
        receiver = (day_index == forward_day + 1) | (day_index == backward_day - 1)
        handed_rows = jnp.where(receiver, handed, handed_rows)
    rows = jnp.stack(
        [
            jnp.where(even_day, own_rows, handed_rows),
            jnp.where(even_day, handed_rows, own_rows),
        ]
    )
    forward_rows = rows[0]
    backward_rows = rows[1]
    both_out = swap_blocks(rows, 2, 1, (2, own_weight.shape[0], per_device))
    forward_out = both_out[0]
    backward_out = both_out[1]
    mass_part = jnp.sum(forward_rows * block_weight * backward_rows, axis=0)
    full_mass = live_all * sum_over_pt(mass_part)
    mass_total = jnp.sum(full_mass)

    cell_total = cell_count[0]
    cell_total_f = cell_total.astype(jnp.float32)
    own_cells = cells[0]
    own_slots = own_cells.shape[1]
    cell_norm = norm_of(own_cells)
    cell_live = (pt_rank * own_slots + jnp.arange(own_slots, dtype=jnp.int32) < cell_total).astype(
        jnp.float32
    )
    cell_span = own_slots // 2
    ratio_rows = 0.0
    for part in range(2):
        part_cells = lax.slice_in_dim(own_cells, part * cell_span, (part + 1) * cell_span, axis=1)
        part_norm = lax.slice_in_dim(cell_norm, part * cell_span, (part + 1) * cell_span)
        fit_kernel = jnp.exp(-squared_dist(day_pts, day_norm, part_cells, part_norm))
        density = jnp.sum(full_mass[:, None] * fit_kernel, axis=0) / mass_total
        part_live = lax.slice_in_dim(cell_live, part * cell_span, (part + 1) * cell_span)
        inverse = part_live / density
        ratio_rows = ratio_rows + jnp.sum(fit_kernel * inverse[None, :], axis=1)
    summed = sum_scatter_over_pt(ratio_rows)
    fit_rows_out = live_own / cell_total_f * summed
    return (forward_out[None], backward_out[None], fit_rows_out[None])


def solution(mesh):
    in_specs = (
        P("day", None, "pt"),
        P("day", None, "pt"),
        P("day", None, "pt"),
        P("day", "pt"),
        P("day"),
        P("day"),
    )
    out_specs = (P("day", None, "pt"), P("day", None, "pt"), P("day", "pt"))
    return jax.shard_map(shards, mesh=mesh, in_specs=in_specs, out_specs=out_specs, check_vma=False)
```

```python
import jax
import jax.numpy as jnp
from jax import lax
from jax.sharding import PartitionSpec as P


def shifted(block, axis, distance):
    devices = range(lax.axis_size(axis))
    route = [(i - distance, i) for i in devices if i - distance in devices]
    return lax.ppermute(block, axis, route)


def swap_blocks(x, take_axis, put_axis, put_shape):
    count = lax.axis_size("pt")
    rank = lax.axis_index("pt")
    take = x.shape[take_axis] // count
    put = put_shape[put_axis] // count
    out = jnp.zeros(put_shape, x.dtype)
    for shift in range(count):
        piece = lax.dynamic_slice_in_dim(x, ((rank + shift) % count) * take, take, take_axis)
        if shift:
            piece = lax.ppermute(piece, "pt", [(i, (i + shift) % count) for i in range(count)])
        out = lax.dynamic_update_slice_in_dim(out, piece, ((rank - shift) % count) * put, put_axis)
    return out


def sum_over_pt(x):
    count = lax.axis_size("pt")
    every = swap_blocks(jnp.broadcast_to(x[None], (count,) + x.shape), 0, 0, (count,) + x.shape)
    return jnp.sum(every, axis=0)


def sum_scatter_over_pt(x):
    count = lax.axis_size("pt")
    every = swap_blocks(x, 0, 0, x.shape)
    return jnp.sum(every.reshape((count, x.shape[0] // count) + x.shape[1:]), axis=0)


def norm_of(coords):
    wide = coords.astype(jnp.float32)
    return jnp.sum(wide * wide, axis=0)


def squared_dist(left_pts, left_norm, right_pts, right_norm):
    inner = lax.dot_general(
        left_pts, right_pts, (((0,), (0,)), ((), ())), preferred_element_type=jnp.float32
    )
    return left_norm[:, None] + right_norm[None, :] - 2.0 * inner


def shards(points, cells, clone_weight, potential, support_count, cell_count):
    pt_rank = lax.axis_index("pt")
    day_index = lax.axis_index("day")
    day_count = lax.axis_size("day")
    own_pts = points[0]
    per_device = own_pts.shape[1]
    day_pts = lax.all_gather(own_pts, "pt", axis=1, tiled=True)
    support_total = day_pts.shape[1]
    own_weight = clone_weight[0] * potential[0][None, :]
    block_rows = own_weight.shape[0] // lax.axis_size("pt")
    block_weight = swap_blocks(own_weight, 0, 1, (block_rows, day_pts.shape[1]))
    live_total = support_count[0].astype(jnp.float32)
    live_all = (jnp.arange(support_total, dtype=jnp.int32) < support_count[0]).astype(jnp.float32)
    live_own = lax.dynamic_slice_in_dim(live_all, pt_rank * per_device, per_device)
    day_norm = norm_of(day_pts)

    def chain_kernel(source_pts):
        dist = squared_dist(source_pts, norm_of(source_pts), day_pts, day_norm)
        return jnp.exp(-dist).astype(jnp.bfloat16)

    half = day_count // 2
    even_day = day_index % 2 == 0
    pair_route = [(d + 1, d) if d % 2 == 0 else (d - 1, d) for d in range(day_count)]
    link_route = [(d - 1, d) if d % 2 == 0 else (d + 1, d) for d in range(1, day_count - 1)]
    other_pts = lax.ppermute(day_pts, "day", pair_route)
    other_kernel = jnp.exp(
        -squared_dist(day_pts, day_norm, other_pts, norm_of(other_pts))
    ).astype(jnp.bfloat16)
    other_weight = lax.ppermute(block_weight, "day", pair_route)
    other_count = lax.ppermute(support_count, "day", pair_route)[0]
    other_total = other_count.astype(jnp.float32)
    other_live = (jnp.arange(support_total, dtype=jnp.int32) < other_count).astype(jnp.float32)
    link_pts = lax.ppermute(day_pts, "day", link_route)

    def settle(values, live, total):
        masked = values * live[None, :]
        return masked * total / jnp.sum(masked, axis=1, keepdims=True)

    seed_rows = jnp.broadcast_to(live_all[None, :], (block_rows, support_total))
    own_rows = seed_rows
    handed_rows = jnp.zeros_like(seed_rows)
    incoming = None
    link_kernel = None
    for round_index in range(half):
        forward_day = 2 * round_index
        backward_day = day_count - 1 - 2 * round_index
        if round_index == 0:
            current = seed_rows
        else:
            current = settle(
                jnp.dot(incoming, link_kernel, preferred_element_type=jnp.float32),
                live_all,
                live_total,
            )
            active = (day_index == forward_day) | (day_index == backward_day)
            own_rows = jnp.where(active, current, own_rows)
        sent = (current * block_weight).astype(jnp.bfloat16)
        following = settle(
            jnp.dot(sent, other_kernel, preferred_element_type=jnp.float32),
            other_live,
            other_total,
        )
        if round_index == 0:
            link_pts = lax.optimization_barrier((link_pts, following))[0]
            link_kernel = chain_kernel(link_pts)
        if round_index < half - 1:
            outgoing = (following * other_weight).astype(jnp.bfloat16)
            incoming = lax.ppermute(
                outgoing, "day", [(forward_day, forward_day + 2), (backward_day, backward_day - 2)]
            )
        handed = lax.ppermute(
            following, "day", [(forward_day, forward_day + 1), (backward_day, backward_day - 1)]
        )
        receiver = (day_index == forward_day + 1) | (day_index == backward_day - 1)
        handed_rows = jnp.where(receiver, handed, handed_rows)
    rows = jnp.stack(
        [
            jnp.where(even_day, own_rows, handed_rows),
            jnp.where(even_day, handed_rows, own_rows),
        ]
    )
    forward_rows = rows[0]
    backward_rows = rows[1]
    both_out = swap_blocks(rows, 2, 1, (2, own_weight.shape[0], per_device))
    forward_out = both_out[0]
    backward_out = both_out[1]
    mass_part = jnp.sum(forward_rows * block_weight * backward_rows, axis=0)
    full_mass = live_all * sum_over_pt(mass_part)
    mass_total = jnp.sum(full_mass)

    cell_total = cell_count[0]
    cell_total_f = cell_total.astype(jnp.float32)
    own_cells = cells[0]
    own_slots = own_cells.shape[1]
    cell_norm = norm_of(own_cells)
    cell_live = (pt_rank * own_slots + jnp.arange(own_slots, dtype=jnp.int32) < cell_total).astype(
        jnp.float32
    )
    cell_parts = 4
    cell_span = own_slots // cell_parts
    ratio_rows = 0.0
    for part in range(cell_parts):
        part_cells = lax.slice_in_dim(own_cells, part * cell_span, (part + 1) * cell_span, axis=1)
        part_norm = lax.slice_in_dim(cell_norm, part * cell_span, (part + 1) * cell_span)
        fit_kernel = jnp.exp(-squared_dist(day_pts, day_norm, part_cells, part_norm))
        density = jnp.sum(full_mass[:, None] * fit_kernel, axis=0) / mass_total
        part_live = lax.slice_in_dim(cell_live, part * cell_span, (part + 1) * cell_span)
        inverse = part_live / density
        ratio_rows = ratio_rows + jnp.sum(fit_kernel * inverse[None, :], axis=1)
    summed = sum_scatter_over_pt(ratio_rows)
    fit_rows_out = live_own / cell_total_f * summed
    return (forward_out[None], backward_out[None], fit_rows_out[None])


def solution(mesh):
    in_specs = (
        P("day", None, "pt"),
        P("day", None, "pt"),
        P("day", None, "pt"),
        P("day", "pt"),
        P("day"),
        P("day"),
    )
    out_specs = (P("day", None, "pt"), P("day", None, "pt"), P("day", "pt"))
    return jax.shard_map(shards, mesh=mesh, in_specs=in_specs, out_specs=out_specs, check_vma=False)
```

```python
import jax
import jax.numpy as jnp
from jax import lax
from jax.sharding import PartitionSpec as P


def shifted(block, axis, distance):
    devices = range(lax.axis_size(axis))
    route = [(i - distance, i) for i in devices if i - distance in devices]
    return lax.ppermute(block, axis, route)


def swap_blocks(x, take_axis, put_axis, put_shape):
    count = lax.axis_size("pt")
    rank = lax.axis_index("pt")
    take = x.shape[take_axis] // count
    put = put_shape[put_axis] // count
    out = jnp.zeros(put_shape, x.dtype)
    for shift in range(count):
        piece = lax.dynamic_slice_in_dim(x, ((rank + shift) % count) * take, take, take_axis)
        if shift:
            piece = lax.ppermute(piece, "pt", [(i, (i + shift) % count) for i in range(count)])
        out = lax.dynamic_update_slice_in_dim(out, piece, ((rank - shift) % count) * put, put_axis)
    return out


def sum_over_pt(x):
    count = lax.axis_size("pt")
    every = swap_blocks(jnp.broadcast_to(x[None], (count,) + x.shape), 0, 0, (count,) + x.shape)
    return jnp.sum(every, axis=0)


def sum_scatter_over_pt(x):
    count = lax.axis_size("pt")
    every = swap_blocks(x, 0, 0, x.shape)
    return jnp.sum(every.reshape((count, x.shape[0] // count) + x.shape[1:]), axis=0)


def norm_of(coords):
    wide = coords.astype(jnp.float32)
    return jnp.sum(wide * wide, axis=0)


def squared_dist(left_pts, left_norm, right_pts, right_norm):
    inner = lax.dot_general(
        left_pts, right_pts, (((0,), (0,)), ((), ())), preferred_element_type=jnp.float32
    )
    return left_norm[:, None] + right_norm[None, :] - 2.0 * inner


def shards(points, cells, clone_weight, potential, support_count, cell_count):
    pt_rank = lax.axis_index("pt")
    day_index = lax.axis_index("day")
    day_count = lax.axis_size("day")
    own_pts = points[0]
    per_device = own_pts.shape[1]
    day_pts = lax.all_gather(own_pts, "pt", axis=1, tiled=True)
    support_total = day_pts.shape[1]
    own_weight = clone_weight[0] * potential[0][None, :]
    block_rows = own_weight.shape[0] // lax.axis_size("pt")
    block_weight = swap_blocks(own_weight, 0, 1, (block_rows, day_pts.shape[1]))
    live_total = support_count[0].astype(jnp.float32)
    live_all = (jnp.arange(support_total, dtype=jnp.int32) < support_count[0]).astype(jnp.float32)
    live_own = lax.dynamic_slice_in_dim(live_all, pt_rank * per_device, per_device)
    day_norm = norm_of(day_pts)

    def chain_kernel(source_pts):
        dist = squared_dist(source_pts, norm_of(source_pts), day_pts, day_norm)
        return jnp.exp(-dist).astype(jnp.bfloat16)

    half = day_count // 2
    even_day = day_index % 2 == 0
    pair_route = [(d + 1, d) if d % 2 == 0 else (d - 1, d) for d in range(day_count)]
    link_route = [(d - 1, d) if d % 2 == 0 else (d + 1, d) for d in range(1, day_count - 1)]
    other_pts = lax.ppermute(day_pts, "day", pair_route)
    other_kernel = jnp.exp(
        -squared_dist(day_pts, day_norm, other_pts, norm_of(other_pts))
    ).astype(jnp.bfloat16)
    other_weight = lax.ppermute(block_weight, "day", pair_route)
    other_count = lax.ppermute(support_count, "day", pair_route)[0]
    other_total = other_count.astype(jnp.float32)
    other_live = (jnp.arange(support_total, dtype=jnp.int32) < other_count).astype(jnp.float32)
    link_pts = lax.ppermute(day_pts, "day", link_route)

    def settle(values, live, total):
        masked = values * live[None, :]
        return masked * total / jnp.sum(masked, axis=1, keepdims=True)

    seed_rows = jnp.broadcast_to(live_all[None, :], (block_rows, support_total))
    own_rows = seed_rows
    handed_rows = jnp.zeros_like(seed_rows)
    incoming = None
    link_kernel = None
    for round_index in range(half):
        forward_day = 2 * round_index
        backward_day = day_count - 1 - 2 * round_index
        if round_index == 0:
            current = seed_rows
        else:
            current = settle(
                jnp.dot(incoming, link_kernel, preferred_element_type=jnp.float32),
                live_all,
                live_total,
            )
            active = (day_index == forward_day) | (day_index == backward_day)
            own_rows = jnp.where(active, current, own_rows)
        sent = (current * block_weight).astype(jnp.bfloat16)
        following = settle(
            jnp.dot(sent, other_kernel, preferred_element_type=jnp.float32),
            other_live,
            other_total,
        )
        if round_index == 0:
            link_pts = lax.optimization_barrier((link_pts, following))[0]
            link_kernel = chain_kernel(link_pts)
        if round_index < half - 1:
            outgoing = (following * other_weight).astype(jnp.bfloat16)
            incoming = lax.ppermute(
                outgoing, "day", [(forward_day, forward_day + 2), (backward_day, backward_day - 2)]
            )
        handed = lax.ppermute(
            following, "day", [(forward_day, forward_day + 1), (backward_day, backward_day - 1)]
        )
        receiver = (day_index == forward_day + 1) | (day_index == backward_day - 1)
        handed_rows = jnp.where(receiver, handed, handed_rows)
    rows = jnp.stack(
        [
            jnp.where(even_day, own_rows, handed_rows),
            jnp.where(even_day, handed_rows, own_rows),
        ]
    )
    forward_rows = rows[0]
    backward_rows = rows[1]
    both_out = swap_blocks(rows, 2, 1, (2, own_weight.shape[0], per_device))
    forward_out = both_out[0]
    backward_out = both_out[1]
    mass_part = jnp.sum(forward_rows * block_weight * backward_rows, axis=0)
    full_mass = live_all * sum_over_pt(mass_part)
    mass_total = jnp.sum(full_mass)

    cell_total = cell_count[0]
    cell_total_f = cell_total.astype(jnp.float32)
    own_cells = cells[0]
    own_slots = own_cells.shape[1]
    cell_norm = norm_of(own_cells)
    cell_live = (pt_rank * own_slots + jnp.arange(own_slots, dtype=jnp.int32) < cell_total).astype(
        jnp.float32
    )
    cell_parts = 8
    cell_span = own_slots // cell_parts
    ratio_rows = 0.0
    for part in range(cell_parts):
        part_cells = lax.slice_in_dim(own_cells, part * cell_span, (part + 1) * cell_span, axis=1)
        part_norm = lax.slice_in_dim(cell_norm, part * cell_span, (part + 1) * cell_span)
        fit_kernel = jnp.exp(-squared_dist(day_pts, day_norm, part_cells, part_norm))
        density = jnp.sum(full_mass[:, None] * fit_kernel, axis=0) / mass_total
        part_live = lax.slice_in_dim(cell_live, part * cell_span, (part + 1) * cell_span)
        inverse = part_live / density
        ratio_rows = ratio_rows + jnp.sum(fit_kernel * inverse[None, :], axis=1)
    summed = sum_scatter_over_pt(ratio_rows)
    fit_rows_out = live_own / cell_total_f * summed
    return (forward_out[None], backward_out[None], fit_rows_out[None])


def solution(mesh):
    in_specs = (
        P("day", None, "pt"),
        P("day", None, "pt"),
        P("day", None, "pt"),
        P("day", "pt"),
        P("day"),
        P("day"),
    )
    out_specs = (P("day", None, "pt"), P("day", None, "pt"), P("day", "pt"))
    return jax.shard_map(shards, mesh=mesh, in_specs=in_specs, out_specs=out_specs, check_vma=False)
```

```python
import jax
import jax.numpy as jnp
from jax import lax
from jax.sharding import PartitionSpec as P


def shifted(block, axis, distance):
    devices = range(lax.axis_size(axis))
    route = [(i - distance, i) for i in devices if i - distance in devices]
    return lax.ppermute(block, axis, route)


def swap_blocks(x, take_axis, put_axis, put_shape):
    count = lax.axis_size("pt")
    rank = lax.axis_index("pt")
    take = x.shape[take_axis] // count
    put = put_shape[put_axis] // count
    out = jnp.zeros(put_shape, x.dtype)
    for shift in range(count):
        piece = lax.dynamic_slice_in_dim(x, ((rank + shift) % count) * take, take, take_axis)
        if shift:
            piece = lax.ppermute(piece, "pt", [(i, (i + shift) % count) for i in range(count)])
        out = lax.dynamic_update_slice_in_dim(out, piece, ((rank - shift) % count) * put, put_axis)
    return out


def sum_over_pt(x):
    count = lax.axis_size("pt")
    every = swap_blocks(jnp.broadcast_to(x[None], (count,) + x.shape), 0, 0, (count,) + x.shape)
    return jnp.sum(every, axis=0)


def sum_scatter_over_pt(x):
    count = lax.axis_size("pt")
    every = swap_blocks(x, 0, 0, x.shape)
    return jnp.sum(every.reshape((count, x.shape[0] // count) + x.shape[1:]), axis=0)


def norm_of(coords):
    wide = coords.astype(jnp.float32)
    return jnp.sum(wide * wide, axis=0)


def squared_dist(left_pts, left_norm, right_pts, right_norm):
    inner = lax.dot_general(
        left_pts, right_pts, (((0,), (0,)), ((), ())), preferred_element_type=jnp.float32
    )
    return left_norm[:, None] + right_norm[None, :] - 2.0 * inner


def shards(points, cells, clone_weight, potential, support_count, cell_count):
    pt_rank = lax.axis_index("pt")
    day_index = lax.axis_index("day")
    day_count = lax.axis_size("day")
    own_pts = points[0]
    per_device = own_pts.shape[1]
    day_pts = lax.all_gather(own_pts, "pt", axis=1, tiled=True)
    support_total = day_pts.shape[1]
    own_weight = clone_weight[0] * potential[0][None, :]
    block_rows = own_weight.shape[0] // lax.axis_size("pt")
    block_weight = swap_blocks(own_weight, 0, 1, (block_rows, day_pts.shape[1]))
    live_total = support_count[0].astype(jnp.float32)
    live_all = (jnp.arange(support_total, dtype=jnp.int32) < support_count[0]).astype(jnp.float32)
    live_own = lax.dynamic_slice_in_dim(live_all, pt_rank * per_device, per_device)
    day_norm = norm_of(day_pts)

    def chain_kernel(source_pts):
        dist = squared_dist(source_pts, norm_of(source_pts), day_pts, day_norm)
        return jnp.exp(-dist).astype(jnp.bfloat16)

    half = day_count // 2
    even_day = day_index % 2 == 0
    pair_route = [(d + 1, d) if d % 2 == 0 else (d - 1, d) for d in range(day_count)]
    link_route = [(d - 1, d) if d % 2 == 0 else (d + 1, d) for d in range(1, day_count - 1)]
    other_pts = lax.ppermute(day_pts, "day", pair_route)
    other_kernel = jnp.exp(
        -squared_dist(day_pts, day_norm, other_pts, norm_of(other_pts))
    ).astype(jnp.bfloat16)
    other_weight = lax.ppermute(block_weight, "day", pair_route)
    other_count = lax.ppermute(support_count, "day", pair_route)[0]
    other_total = other_count.astype(jnp.float32)
    other_live = (jnp.arange(support_total, dtype=jnp.int32) < other_count).astype(jnp.float32)
    link_pts = lax.ppermute(day_pts, "day", link_route)

    def settle(values, live, total):
        masked = values * live[None, :]
        return masked * total / jnp.sum(masked, axis=1, keepdims=True)

    seed_rows = jnp.broadcast_to(live_all[None, :], (block_rows, support_total))
    own_rows = seed_rows
    handed_rows = jnp.zeros_like(seed_rows)
    incoming = None
    link_kernel = None
    for round_index in range(half):
        forward_day = 2 * round_index
        backward_day = day_count - 1 - 2 * round_index
        if round_index == 0:
            current = seed_rows
        else:
            current = settle(
                jnp.dot(incoming, link_kernel, preferred_element_type=jnp.float32),
                live_all,
                live_total,
            )
            active = (day_index == forward_day) | (day_index == backward_day)
            own_rows = jnp.where(active, current, own_rows)
        sent = (current * block_weight).astype(jnp.bfloat16)
        following = settle(
            jnp.dot(sent, other_kernel, preferred_element_type=jnp.float32),
            other_live,
            other_total,
        )
        if round_index == 0:
            link_pts = lax.optimization_barrier((link_pts, following))[0]
            link_kernel = chain_kernel(link_pts)
        if round_index < half - 1:
            outgoing = (following * other_weight).astype(jnp.bfloat16)
            incoming = lax.ppermute(
                outgoing, "day", [(forward_day, forward_day + 2), (backward_day, backward_day - 2)]
            )
        handed = lax.ppermute(
            following, "day", [(forward_day, forward_day + 1), (backward_day, backward_day - 1)]
        )
        receiver = (day_index == forward_day + 1) | (day_index == backward_day - 1)
        handed_rows = jnp.where(receiver, handed, handed_rows)
    rows = jnp.stack(
        [
            jnp.where(even_day, own_rows, handed_rows),
            jnp.where(even_day, handed_rows, own_rows),
        ]
    )
    forward_rows = rows[0]
    backward_rows = rows[1]
    both_out = swap_blocks(rows, 2, 1, (2, own_weight.shape[0], per_device))
    forward_out = both_out[0]
    backward_out = both_out[1]
    mass_part = jnp.sum(forward_rows * block_weight * backward_rows, axis=0)
    full_mass = live_all * sum_over_pt(mass_part)
    full_mass, both_out = lax.optimization_barrier((full_mass, both_out))
    forward_out = both_out[0]
    backward_out = both_out[1]
    mass_total = jnp.sum(full_mass)

    cell_total = cell_count[0]
    cell_total_f = cell_total.astype(jnp.float32)
    own_cells = cells[0]
    own_slots = own_cells.shape[1]
    cell_norm = norm_of(own_cells)
    cell_live = (pt_rank * own_slots + jnp.arange(own_slots, dtype=jnp.int32) < cell_total).astype(
        jnp.float32
    )
    cell_parts = 4
    cell_span = own_slots // cell_parts
    ratio_rows = 0.0
    for part in range(cell_parts):
        part_cells = lax.slice_in_dim(own_cells, part * cell_span, (part + 1) * cell_span, axis=1)
        part_norm = lax.slice_in_dim(cell_norm, part * cell_span, (part + 1) * cell_span)
        fit_kernel = jnp.exp(-squared_dist(day_pts, day_norm, part_cells, part_norm))
        density = jnp.sum(full_mass[:, None] * fit_kernel, axis=0) / mass_total
        part_live = lax.slice_in_dim(cell_live, part * cell_span, (part + 1) * cell_span)
        inverse = part_live / density
        ratio_rows = ratio_rows + jnp.sum(fit_kernel * inverse[None, :], axis=1)
    summed = sum_scatter_over_pt(ratio_rows)
    fit_rows_out = live_own / cell_total_f * summed
    return (forward_out[None], backward_out[None], fit_rows_out[None])


def solution(mesh):
    in_specs = (
        P("day", None, "pt"),
        P("day", None, "pt"),
        P("day", None, "pt"),
        P("day", "pt"),
        P("day"),
        P("day"),
    )
    out_specs = (P("day", None, "pt"), P("day", None, "pt"), P("day", "pt"))
    return jax.shard_map(shards, mesh=mesh, in_specs=in_specs, out_specs=out_specs, check_vma=False)
```

```python
import jax
import jax.numpy as jnp
from jax import lax
from jax.sharding import PartitionSpec as P


def shifted(block, axis, distance):
    devices = range(lax.axis_size(axis))
    route = [(i - distance, i) for i in devices if i - distance in devices]
    return lax.ppermute(block, axis, route)


def swap_blocks(x, take_axis, put_axis, put_shape):
    count = lax.axis_size("pt")
    rank = lax.axis_index("pt")
    take = x.shape[take_axis] // count
    put = put_shape[put_axis] // count
    out = jnp.zeros(put_shape, x.dtype)
    for shift in range(count):
        piece = lax.dynamic_slice_in_dim(x, ((rank + shift) % count) * take, take, take_axis)
        if shift:
            piece = lax.ppermute(piece, "pt", [(i, (i + shift) % count) for i in range(count)])
        out = lax.dynamic_update_slice_in_dim(out, piece, ((rank - shift) % count) * put, put_axis)
    return out


def sum_over_pt(x):
    count = lax.axis_size("pt")
    every = swap_blocks(jnp.broadcast_to(x[None], (count,) + x.shape), 0, 0, (count,) + x.shape)
    return jnp.sum(every, axis=0)


def sum_scatter_over_pt(x):
    count = lax.axis_size("pt")
    every = swap_blocks(x, 0, 0, x.shape)
    return jnp.sum(every.reshape((count, x.shape[0] // count) + x.shape[1:]), axis=0)


def norm_of(coords):
    wide = coords.astype(jnp.float32)
    return jnp.sum(wide * wide, axis=0)


def squared_dist(left_pts, left_norm, right_pts, right_norm):
    inner = lax.dot_general(
        left_pts, right_pts, (((0,), (0,)), ((), ())), preferred_element_type=jnp.float32
    )
    return left_norm[:, None] + right_norm[None, :] - 2.0 * inner


def shards(points, cells, clone_weight, potential, support_count, cell_count):
    pt_rank = lax.axis_index("pt")
    day_index = lax.axis_index("day")
    day_count = lax.axis_size("day")
    own_pts = points[0]
    per_device = own_pts.shape[1]
    day_pts = lax.all_gather(own_pts, "pt", axis=1, tiled=True)
    support_total = day_pts.shape[1]
    own_weight = clone_weight[0] * potential[0][None, :]
    block_rows = own_weight.shape[0] // lax.axis_size("pt")
    block_weight = swap_blocks(own_weight, 0, 1, (block_rows, day_pts.shape[1]))
    live_total = support_count[0].astype(jnp.float32)
    live_all = (jnp.arange(support_total, dtype=jnp.int32) < support_count[0]).astype(jnp.float32)
    live_own = lax.dynamic_slice_in_dim(live_all, pt_rank * per_device, per_device)
    day_norm = norm_of(day_pts)

    def chain_kernel(source_pts):
        dist = squared_dist(source_pts, norm_of(source_pts), day_pts, day_norm)
        return jnp.exp(-dist).astype(jnp.bfloat16)

    half = day_count // 2
    even_day = day_index % 2 == 0
    pair_route = [(d + 1, d) if d % 2 == 0 else (d - 1, d) for d in range(day_count)]
    link_route = [(d - 1, d) if d % 2 == 0 else (d + 1, d) for d in range(1, day_count - 1)]
    other_pts = lax.ppermute(day_pts, "day", pair_route)
    other_kernel = jnp.exp(
        -squared_dist(day_pts, day_norm, other_pts, norm_of(other_pts))
    ).astype(jnp.bfloat16)
    other_weight = lax.ppermute(block_weight, "day", pair_route)
    other_count = lax.ppermute(support_count, "day", pair_route)[0]
    other_total = other_count.astype(jnp.float32)
    other_live = (jnp.arange(support_total, dtype=jnp.int32) < other_count).astype(jnp.float32)
    link_pts = lax.ppermute(day_pts, "day", link_route)

    def settle(values, live, total):
        masked = values * live[None, :]
        return masked * total / jnp.sum(masked, axis=1, keepdims=True)

    seed_rows = jnp.broadcast_to(live_all[None, :], (block_rows, support_total))
    own_rows = seed_rows
    handed_rows = jnp.zeros_like(seed_rows)
    incoming = None
    link_kernel = None
    for round_index in range(half):
        forward_day = 2 * round_index
        backward_day = day_count - 1 - 2 * round_index
        if round_index == 0:
            current = seed_rows
        else:
            current = settle(
                jnp.dot(incoming, link_kernel, preferred_element_type=jnp.float32),
                live_all,
                live_total,
            )
            active = (day_index == forward_day) | (day_index == backward_day)
            own_rows = jnp.where(active, current, own_rows)
        sent = (current * block_weight).astype(jnp.bfloat16)
        following = settle(
            jnp.dot(sent, other_kernel, preferred_element_type=jnp.float32),
            other_live,
            other_total,
        )
        if round_index == 0:
            link_kernel = chain_kernel(link_pts)
        if round_index < half - 1:
            outgoing = (following * other_weight).astype(jnp.bfloat16)
            incoming = lax.ppermute(
                outgoing, "day", [(forward_day, forward_day + 2), (backward_day, backward_day - 2)]
            )
        handed = lax.ppermute(
            following, "day", [(forward_day, forward_day + 1), (backward_day, backward_day - 1)]
        )
        receiver = (day_index == forward_day + 1) | (day_index == backward_day - 1)
        handed_rows = jnp.where(receiver, handed, handed_rows)
    rows = jnp.stack(
        [
            jnp.where(even_day, own_rows, handed_rows),
            jnp.where(even_day, handed_rows, own_rows),
        ]
    )
    forward_rows = rows[0]
    backward_rows = rows[1]
    both_out = swap_blocks(rows, 2, 1, (2, own_weight.shape[0], per_device))
    forward_out = both_out[0]
    backward_out = both_out[1]
    mass_part = jnp.sum(forward_rows * block_weight * backward_rows, axis=0)
    full_mass = live_all * sum_over_pt(mass_part)
    mass_total = jnp.sum(full_mass)

    cell_total = cell_count[0]
    cell_total_f = cell_total.astype(jnp.float32)
    own_cells = cells[0]
    own_slots = own_cells.shape[1]
    cell_norm = norm_of(own_cells)
    cell_live = (pt_rank * own_slots + jnp.arange(own_slots, dtype=jnp.int32) < cell_total).astype(
        jnp.float32
    )
    cell_parts = 4
    cell_span = own_slots // cell_parts
    ratio_rows = 0.0
    for part in range(cell_parts):
        part_cells = lax.slice_in_dim(own_cells, part * cell_span, (part + 1) * cell_span, axis=1)
        part_norm = lax.slice_in_dim(cell_norm, part * cell_span, (part + 1) * cell_span)
        fit_kernel = jnp.exp(-squared_dist(day_pts, day_norm, part_cells, part_norm))
        density = jnp.sum(full_mass[:, None] * fit_kernel, axis=0) / mass_total
        part_live = lax.slice_in_dim(cell_live, part * cell_span, (part + 1) * cell_span)
        inverse = part_live / density
        ratio_rows = ratio_rows + jnp.sum(fit_kernel * inverse[None, :], axis=1)
    summed = sum_scatter_over_pt(ratio_rows)
    fit_rows_out = live_own / cell_total_f * summed
    return (forward_out[None], backward_out[None], fit_rows_out[None])


def solution(mesh):
    in_specs = (
        P("day", None, "pt"),
        P("day", None, "pt"),
        P("day", None, "pt"),
        P("day", "pt"),
        P("day"),
        P("day"),
    )
    out_specs = (P("day", None, "pt"), P("day", None, "pt"), P("day", "pt"))
    return jax.shard_map(shards, mesh=mesh, in_specs=in_specs, out_specs=out_specs, check_vma=False)
```

```python
import jax
import jax.numpy as jnp
from jax import lax
from jax.sharding import PartitionSpec as P


def shifted(block, axis, distance):
    devices = range(lax.axis_size(axis))
    route = [(i - distance, i) for i in devices if i - distance in devices]
    return lax.ppermute(block, axis, route)


def swap_blocks(x, take_axis, put_axis, put_shape):
    count = lax.axis_size("pt")
    rank = lax.axis_index("pt")
    take = x.shape[take_axis] // count
    put = put_shape[put_axis] // count
    out = jnp.zeros(put_shape, x.dtype)
    for shift in range(count):
        piece = lax.dynamic_slice_in_dim(x, ((rank + shift) % count) * take, take, take_axis)
        if shift:
            piece = lax.ppermute(piece, "pt", [(i, (i + shift) % count) for i in range(count)])
        out = lax.dynamic_update_slice_in_dim(out, piece, ((rank - shift) % count) * put, put_axis)
    return out


def gather_over_pt(x, axis):
    count = lax.axis_size("pt")
    rank = lax.axis_index("pt")
    shape = list(x.shape)
    shape[axis] *= count
    out = jnp.zeros(shape, x.dtype)
    for shift in range(count):
        piece = x if shift == 0 else lax.ppermute(
            x, "pt", [((i + shift) % count, i) for i in range(count)]
        )
        out = lax.dynamic_update_slice_in_dim(
            out, piece, ((rank + shift) % count) * x.shape[axis], axis
        )
    return out


def sum_over_pt(x):
    count = lax.axis_size("pt")
    every = swap_blocks(jnp.broadcast_to(x[None], (count,) + x.shape), 0, 0, (count,) + x.shape)
    return jnp.sum(every, axis=0)


def sum_scatter_over_pt(x):
    count = lax.axis_size("pt")
    every = swap_blocks(x, 0, 0, x.shape)
    return jnp.sum(every.reshape((count, x.shape[0] // count) + x.shape[1:]), axis=0)


def norm_of(coords):
    wide = coords.astype(jnp.float32)
    return jnp.sum(wide * wide, axis=0)


def squared_dist(left_pts, left_norm, right_pts, right_norm):
    inner = lax.dot_general(
        left_pts, right_pts, (((0,), (0,)), ((), ())), preferred_element_type=jnp.float32
    )
    return left_norm[:, None] + right_norm[None, :] - 2.0 * inner


def shards(points, cells, clone_weight, potential, support_count, cell_count):
    pt_rank = lax.axis_index("pt")
    day_index = lax.axis_index("day")
    day_count = lax.axis_size("day")
    own_pts = points[0]
    per_device = own_pts.shape[1]
    day_pts = gather_over_pt(own_pts, 1)
    support_total = day_pts.shape[1]
    own_weight = clone_weight[0] * potential[0][None, :]
    block_rows = own_weight.shape[0] // lax.axis_size("pt")
    block_weight = swap_blocks(own_weight, 0, 1, (block_rows, day_pts.shape[1]))
    live_total = support_count[0].astype(jnp.float32)
    live_all = (jnp.arange(support_total, dtype=jnp.int32) < support_count[0]).astype(jnp.float32)
    live_own = lax.dynamic_slice_in_dim(live_all, pt_rank * per_device, per_device)
    day_norm = norm_of(day_pts)

    def chain_kernel(source_pts):
        dist = squared_dist(source_pts, norm_of(source_pts), day_pts, day_norm)
        return jnp.exp(-dist).astype(jnp.bfloat16)

    half = day_count // 2
    even_day = day_index % 2 == 0
    pair_route = [(d + 1, d) if d % 2 == 0 else (d - 1, d) for d in range(day_count)]
    link_route = [(d - 1, d) if d % 2 == 0 else (d + 1, d) for d in range(1, day_count - 1)]
    other_pts = lax.ppermute(day_pts, "day", pair_route)
    other_kernel = jnp.exp(
        -squared_dist(day_pts, day_norm, other_pts, norm_of(other_pts))
    ).astype(jnp.bfloat16)
    other_weight = lax.ppermute(block_weight, "day", pair_route)
    other_count = lax.ppermute(support_count, "day", pair_route)[0]
    other_total = other_count.astype(jnp.float32)
    other_live = (jnp.arange(support_total, dtype=jnp.int32) < other_count).astype(jnp.float32)
    link_pts = lax.ppermute(day_pts, "day", link_route)

    def settle(values, live, total):
        masked = values * live[None, :]
        return masked * total / jnp.sum(masked, axis=1, keepdims=True)

    seed_rows = jnp.broadcast_to(live_all[None, :], (block_rows, support_total))
    own_rows = seed_rows
    handed_rows = jnp.zeros_like(seed_rows)
    incoming = None
    link_kernel = None
    for round_index in range(half):
        forward_day = 2 * round_index
        backward_day = day_count - 1 - 2 * round_index
        if round_index == 0:
            current = seed_rows
        else:
            current = settle(
                jnp.dot(incoming, link_kernel, preferred_element_type=jnp.float32),
                live_all,
                live_total,
            )
            active = (day_index == forward_day) | (day_index == backward_day)
            own_rows = jnp.where(active, current, own_rows)
        sent = (current * block_weight).astype(jnp.bfloat16)
        following = settle(
            jnp.dot(sent, other_kernel, preferred_element_type=jnp.float32),
            other_live,
            other_total,
        )
        if round_index == 0:
            link_kernel = chain_kernel(link_pts)
        if round_index < half - 1:
            outgoing = (following * other_weight).astype(jnp.bfloat16)
            incoming = lax.ppermute(
                outgoing, "day", [(forward_day, forward_day + 2), (backward_day, backward_day - 2)]
            )
        handed = lax.ppermute(
            following, "day", [(forward_day, forward_day + 1), (backward_day, backward_day - 1)]
        )
        receiver = (day_index == forward_day + 1) | (day_index == backward_day - 1)
        handed_rows = jnp.where(receiver, handed, handed_rows)
    rows = jnp.stack(
        [
            jnp.where(even_day, own_rows, handed_rows),
            jnp.where(even_day, handed_rows, own_rows),
        ]
    )
    forward_rows = rows[0]
    backward_rows = rows[1]
    both_out = swap_blocks(rows, 2, 1, (2, own_weight.shape[0], per_device))
    forward_out = both_out[0]
    backward_out = both_out[1]
    mass_part = jnp.sum(forward_rows * block_weight * backward_rows, axis=0)
    full_mass = live_all * sum_over_pt(mass_part)
    mass_total = jnp.sum(full_mass)

    cell_total = cell_count[0]
    cell_total_f = cell_total.astype(jnp.float32)
    own_cells = cells[0]
    own_slots = own_cells.shape[1]
    cell_norm = norm_of(own_cells)
    cell_live = (pt_rank * own_slots + jnp.arange(own_slots, dtype=jnp.int32) < cell_total).astype(
        jnp.float32
    )
    cell_parts = 4
    cell_span = own_slots // cell_parts
    ratio_rows = 0.0
    for part in range(cell_parts):
        part_cells = lax.slice_in_dim(own_cells, part * cell_span, (part + 1) * cell_span, axis=1)
        part_norm = lax.slice_in_dim(cell_norm, part * cell_span, (part + 1) * cell_span)
        fit_kernel = jnp.exp(-squared_dist(day_pts, day_norm, part_cells, part_norm))
        density = jnp.sum(full_mass[:, None] * fit_kernel, axis=0) / mass_total
        part_live = lax.slice_in_dim(cell_live, part * cell_span, (part + 1) * cell_span)
        inverse = part_live / density
        ratio_rows = ratio_rows + jnp.sum(fit_kernel * inverse[None, :], axis=1)
    summed = sum_scatter_over_pt(ratio_rows)
    fit_rows_out = live_own / cell_total_f * summed
    return (forward_out[None], backward_out[None], fit_rows_out[None])


def solution(mesh):
    in_specs = (
        P("day", None, "pt"),
        P("day", None, "pt"),
        P("day", None, "pt"),
        P("day", "pt"),
        P("day"),
        P("day"),
    )
    out_specs = (P("day", None, "pt"), P("day", None, "pt"), P("day", "pt"))
    return jax.shard_map(shards, mesh=mesh, in_specs=in_specs, out_specs=out_specs, check_vma=False)
```
